512 devices in a mesh: dom: 64 (over z, y), feat: 8 (over x, core).
Axes of the slice: x: 4, y: 8, z: 8, core: 2. Of those that a mesh axis runs over, the one named last changes fastest.
Arguments:
- features: bfloat16 [32768, 1024], P('dom', 'feat'), may hold values from -6 to 6
- degree: int32 [32768], P('dom'), may hold values from 4 to 39
- hub_ids: int32 [128], P('dom'), may hold values from 0 to 511
- hub_adjacency: bfloat16 [32768, 128], P('dom'), may hold values from 0 to 1
- local_rows: int32 [512], P('dom'), may hold values from 0 to 3
- local_cols: int32 [512], P('dom'), may hold values from 0 to 3
- local_tiles: bfloat16 [512, 128, 128], P('dom'), may hold values from 0 to 1
- out_dest: int32 [4096, 1], P('dom'), may hold values from 0 to 63; in each aligned block of 64 rows (0 to 63, 64 to 127, ...) at most 2 rows name the same one
- out_src: int32 [4096], P('dom'), may hold values from 0 to 3
- out_tiles: bfloat16 [4096, 128, 128], P('dom'), may hold values from 0 to 1
- recv_target: int32 [64, 64, 2], P('dom'), may hold values from 0 to 3
- w_self: bfloat16 [2, 1024, 1024], P(None, None, 'feat'), may hold values from -0.1875 to 0.1875
- w_neigh: bfloat16 [2, 1024, 1024], P(None, None, 'feat'), may hold values from -0.1875 to 0.1875
- gains: bfloat16 [2, 1024], P(None, 'feat'), may hold values from 0.099609375 to 1.8984375
Outputs:
- embeddings: bfloat16 [32768, 1024], P('dom', 'feat')
The draws below stay inside these ranges and needn't reach their ends.
Inputs may be any that keep to these rules, and one draw needn't show every extreme that they name: `hub_ids`: hub j is owned by partition j // 2; its entry is its row within that partition's range. `out_dest`: among the 64 tiles of one partition no reader is named more than 2 times; some reader is named exactly 2 times. recv_target[q, s, c] is the row block of q that the c-th tile sent by s to q lands on; entries past the number of tiles s sends to q are unused.
All inputs are finite; a program needn't handle non-finite values.
Results may differ from the reference program's by a relative error of at most 0.0037.
The reference program's roundings to bfloat16 on the way count: a program that leaves them out, or rounds other values in their place, can miss the bound.
Values may be sent and summed in bfloat16 or wider, within the bound.
No kernel may reach another device: no remote copies, remote signals or barrier semaphores. Data moves between devices by JAX's collectives and lax.ppermute only.
A program may use at most 64 MiB of HBM per device.

```python
import math
import jax
import jax.numpy as jnp
import numpy as np
from jax import lax

D = 1024
BLK = 128
NB = 4
HUB_DEV = 2
LT = 8
CAP = 2
LAYERS = 2
V_DEV = 512
HUBS = 128
NOUT = 64
ROWS = 32768
N_DOM = 64


def with_ends(array, own_key, smallest, high):
    longest = array.shape.index(max(array.shape))
    spots = []
    for shift in (0, 1):
        where = [jax.random.randint(jax.random.fold_in(own_key, axis), (), 0, length) for axis, length in enumerate(array.shape)]
        where[longest] = (where[longest] + shift) % array.shape[longest]
        spots.append(tuple(where))
    return array.at[spots[0]].set(smallest).at[spots[1]].set(high)


def levels(key, extent, shards, smallest, largest):
    level = 1.0
    for axis_at, shards_of in shards:
        draws = jax.random.uniform(jax.random.fold_in(jax.random.fold_in(key, 6), axis_at), (shards_of,), jnp.float32, smallest / len(shards), largest / len(shards))
        level = level * jnp.repeat(jnp.exp(draws), extent[axis_at] // shards_of).reshape((-1,) + (1,) * (len(extent) - 1 - axis_at))
    return level


def routed_block(rng, own, number, rows, number_of, top, most, skew):
    sequence = jax.random.permutation(rng, number_of)
    crowded, common = load_shares(number_of, rows * top, most, skew, True), load_shares(number_of, rows * top, most, skew, False)
    places = jnp.arange(number_of)

    def named(lengths, rotation):
        used = int((lengths > 0).sum())
        fixed = max(1, used // 4)
        moved = fixed + (places - fixed + rotation * (used - fixed)) % max(1, number_of - fixed)
        return jnp.zeros((number_of,), jnp.int32).at[sequence[jnp.where(places < fixed, places, moved)]].set(jnp.asarray(lengths, jnp.int32))

    lengths = jnp.where(number % 4 == 0, named(crowded, number // 4), named(common, number - number // 4 - 1))
    mixed = jax.random.permutation(jax.random.fold_in(own, 3), number_of)
    giver, taker = mixed[0:number_of // 2 * 2:2], mixed[1:number_of // 2 * 2:2]
    slack = jnp.minimum(lengths[giver] - 1, most - lengths[taker]) // 2
    slack = jnp.where((giver == sequence[0]) | (taker == sequence[0]) | (lengths[taker] == 0), 0, jnp.maximum(slack, 0))
    moved = jax.random.randint(jax.random.fold_in(own, 4), (number_of // 2,), 0, 1 << 20) % (slack + 1)
    lengths = lengths.at[giver].add(-moved).at[taker].add(moved)
    labels = jnp.searchsorted(jnp.cumsum(lengths), jnp.arange(rows * top), side="right").astype(jnp.int32)
    table = labels.reshape(top, rows).T
    table = table[jax.random.permutation(jax.random.fold_in(own, 1), rows)]
    rotation = jax.random.randint(jax.random.fold_in(own, 2), (rows, 1), 0, top)
    return jnp.take_along_axis(table, (jnp.arange(top)[None, :] + rotation) % top, axis=1)


def load_shares(amount, total, reach, slope, full):
    loads = [(1 << 20) // math.isqrt(rank ** slope) + 1 for rank in range(1, amount + 1)]
    largest = reach if full else min(reach, max(-(-total // amount), total * loads[0] // sum(loads)))
    least = 1 if total - largest >= amount - 1 else 0
    given, spare = [largest] + [least] * (amount - 1), total - largest - least * (amount - 1)
    while spare > 0:
        movable = [i for i in range(1, amount) if given[i] < largest] or [i for i in range(1, amount) if given[i] < reach]
        mass, budget = sum([loads[i] for i in movable]), spare
        for i in movable:
            extra = min(reach - given[i], max(1, budget * loads[i] // mass), spare)
            given[i] = given[i] + extra
            spare = spare - extra
    return np.array(given)


def gaussian(rng, extent, scale, bound, cuts=(), kind=jnp.bfloat16):
    entries = scale * jax.random.normal(rng, extent, jnp.float32)
    if cuts:
        entries = entries * levels(rng, extent, cuts, -0.22, 0.18)
    return jnp.clip(entries, -bound, bound).astype(kind)


def setup_inputs(seed: int = 0) -> dict:
    arg_keys = jax.random.split(jax.random.key(seed), 15)
    features = gaussian(arg_keys[0], (ROWS, D), 1.0, 6.0, ((0, 64), (1, 8)))
    degree = with_ends(jax.random.randint(arg_keys[1], (ROWS,), 4, 40), jax.random.fold_in(arg_keys[1], 1), 4, 39).astype(jnp.int32)
    hub_ids = with_ends(jax.random.randint(arg_keys[2], (HUBS,), 0, V_DEV), jax.random.fold_in(arg_keys[2], 1), 0, V_DEV - 1).astype(jnp.int32)
    hub_adjacency = jnp.clip(1.0 * jax.random.uniform(arg_keys[3], (ROWS, HUBS), jnp.float32) ** levels(arg_keys[3], (ROWS, HUBS), ((0, 64),), -0.2, 0.2), 0.0, 1.0).astype(jnp.bfloat16)
    local_rows = with_ends(jax.random.randint(arg_keys[4], (N_DOM * LT,), 0, NB), jax.random.fold_in(arg_keys[4], 1), 0, NB - 1).astype(jnp.int32)
    local_cols = with_ends(jax.random.randint(arg_keys[5], (N_DOM * LT,), 0, NB), jax.random.fold_in(arg_keys[5], 1), 0, NB - 1).astype(jnp.int32)
    local_tiles = jnp.clip(1.0 * jax.random.uniform(arg_keys[6], (N_DOM * LT, BLK, BLK), jnp.float32) ** levels(arg_keys[6], (N_DOM * LT, BLK, BLK), ((0, 64),), -0.2, 0.2), 0.0, 1.0).astype(jnp.bfloat16)
    out_dest_keys = jax.random.split(jax.random.fold_in(arg_keys[7], 1), (N_DOM * NOUT) // NOUT)
    out_dest_turns = jax.random.permutation(jax.random.fold_in(arg_keys[7], 3), (N_DOM * NOUT) // NOUT)
    out_dest = jax.vmap(lambda own, number: routed_block(jax.random.fold_in(arg_keys[7], 2), own, number, NOUT, N_DOM, 1, CAP, 2))(out_dest_keys, out_dest_turns).reshape((N_DOM * NOUT, 1))
    out_src = with_ends(jax.random.randint(arg_keys[8], (N_DOM * NOUT,), 0, NB), jax.random.fold_in(arg_keys[8], 1), 0, NB - 1).astype(jnp.int32)
    out_tiles = jnp.clip(1.0 * jax.random.uniform(arg_keys[9], (N_DOM * NOUT, BLK, BLK), jnp.float32) ** levels(arg_keys[9], (N_DOM * NOUT, BLK, BLK), ((0, 64),), -0.2, 0.2), 0.0, 1.0).astype(jnp.bfloat16)
    recv_target = with_ends(jax.random.randint(arg_keys[10], (N_DOM, N_DOM, CAP), 0, NB), jax.random.fold_in(arg_keys[10], 1), 0, NB - 1).astype(jnp.int32)
    w_self = gaussian(arg_keys[11], (LAYERS, D, D), D ** -0.5, 0.1875, ((2, 8),))
    w_neigh = gaussian(arg_keys[12], (LAYERS, D, D), D ** -0.5, 0.1875, ((2, 8),))
    gains = jnp.clip(1.0 + 0.18 * jax.random.normal(arg_keys[13], (LAYERS, D), jnp.float32), 0.099609375, 1.8984375).astype(jnp.bfloat16)
    return dict(features=features, degree=degree, hub_ids=hub_ids, hub_adjacency=hub_adjacency, local_rows=local_rows, local_cols=local_cols, local_tiles=local_tiles, out_dest=out_dest, out_src=out_src, out_tiles=out_tiles, recv_target=recv_target, w_self=w_self, w_neigh=w_neigh, gains=gains)


EPSILON = 1e-06

def slot_ranks(destination):
    tile_count = destination.shape[0]
    positions = jnp.arange(tile_count, dtype=jnp.int32)
    matches = (destination[None, :] == destination[:, None]) & (positions[None, :] < positions[:, None])
    return lax.optimization_barrier(jnp.sum(matches.astype(jnp.int32), axis=1)).astype(jnp.int32)

def aggregate(inputs, degree, hub_ids, hub_adjacency, local_rows, local_cols, local_tiles, out_dest, out_src, out_tiles, recv_target):
    width = inputs.shape[1]
    blocks = inputs.reshape(N_DOM, NB, BLK, width)
    owners = jnp.arange(HUBS, dtype=jnp.int32) // HUB_DEV
    hub_rows = inputs[(owners * V_DEV + hub_ids).astype(jnp.int32)]
    from_hubs = jnp.dot(hub_adjacency, hub_rows, preferred_element_type=jnp.float32)

    def local_part(packed):
        own_blocks, rows_of, cols_of, tiles_of = packed
        products = jnp.einsum('trs,tsd->trd', tiles_of.astype(jnp.float32), own_blocks[cols_of].astype(jnp.float32))
        return jnp.zeros((NB, BLK, width), jnp.float32).at[rows_of].add(products)
    from_local = lax.map(local_part, (blocks, local_rows.reshape(N_DOM, LT), local_cols.reshape(N_DOM, LT), local_tiles.reshape(N_DOM, LT, BLK, BLK)))

    def send_part(summed, packed):
        sender, destination, sources, tiles_of = packed
        sender_blocks = blocks[sender]
        products = jnp.einsum('trs,tsd->trd', tiles_of.astype(jnp.float32), sender_blocks[sources].astype(jnp.float32)).astype(jnp.bfloat16)
        ranks = slot_ranks(destination)
        targets = recv_target[destination, sender, ranks].astype(jnp.int32)
        firsts = (destination * V_DEV + targets * BLK).astype(jnp.int32)
        row_index = (firsts[:, None] + jnp.arange(BLK, dtype=jnp.int32)[None, :]).reshape(-1)
        summed = summed.at[row_index].add(products.reshape(-1, width).astype(jnp.float32))
        return (summed, jnp.zeros((), jnp.float32))
    scanned = lax.scan(send_part, jnp.zeros((N_DOM * V_DEV, width), jnp.float32), (jnp.arange(N_DOM, dtype=jnp.int32), out_dest.reshape(N_DOM, NOUT), out_src.reshape(N_DOM, NOUT), out_tiles.reshape(N_DOM, NOUT, BLK, BLK)))
    summed = scanned[0] + from_local.reshape(N_DOM * V_DEV, width) + from_hubs
    return (summed / degree.astype(jnp.float32)[:, None]).astype(jnp.bfloat16)

def mix(inputs, neighbours, self_weight, neigh_weight, gain):
    mixed = jnp.dot(inputs, self_weight, preferred_element_type=jnp.float32) + jnp.dot(neighbours, neigh_weight, preferred_element_type=jnp.float32)
    rectified = jnp.maximum(mixed, 0.0)
    squares = lax.optimization_barrier(jnp.sum(rectified * rectified, axis=1, keepdims=True)) / D
    return (gain.astype(jnp.float32)[None, :] * rectified * lax.rsqrt(squares + EPSILON)).astype(jnp.bfloat16)

def reference(features, degree, hub_ids, hub_adjacency, local_rows, local_cols, local_tiles, out_dest, out_src, out_tiles, recv_target, w_self, w_neigh, gains):
    current = features
    for layer_idx in range(LAYERS):
        neighbours = aggregate(current, degree, hub_ids, hub_adjacency, local_rows, local_cols, local_tiles, out_dest[:, 0], out_src, out_tiles, recv_target)
        current = mix(current, neighbours, w_self[layer_idx], w_neigh[layer_idx], gains[layer_idx])
    return current
```

```python
import jax
import jax.numpy as jnp
from jax import lax
from jax.sharding import PartitionSpec as P

EPSILON = 1e-06
HUB_PAD = 16


def routing(out_dest, recv_target, block_count, node_count):
    capacity = recv_target.shape[2]
    destination = out_dest[:, 0]
    positions = jnp.arange(destination.shape[0], dtype=jnp.int32)
    matches = (destination[None, :] == destination[:, None]) & (
        positions[None, :] < positions[:, None]
    )
    slot_rank = jnp.sum(matches.astype(jnp.int32), axis=1)
    slots = destination * capacity + slot_rank
    slot_ids = jnp.arange(node_count * capacity, dtype=jnp.int32)
    placing = (slot_ids[:, None] == slots[None, :]).astype(jnp.bfloat16)
    targets = recv_target[0].reshape(-1)
    block_ids = jnp.arange(block_count, dtype=jnp.int32)
    landing = (targets[None, :] == block_ids[:, None]).astype(jnp.bfloat16)
    return placing, landing


def aggregate(
    inputs,
    degree,
    hub_ids,
    hub_adjacency,
    local_rows,
    local_cols,
    local_tiles,
    out_src,
    out_tiles,
    placing,
    landing,
):
    vertex_count, col_count = inputs.shape
    tile_side = local_tiles.shape[1]
    block_count = vertex_count // tile_side
    node_count = lax.axis_size("dom")
    slot_count = placing.shape[0]
    capacity = slot_count // node_count
    hub_count = hub_ids.shape[0]
    blocks = inputs.reshape(block_count, tile_side, col_count)
    block_ids = jnp.arange(block_count, dtype=jnp.int32)
    partials = jnp.einsum(
        "trs,tsd->trd", out_tiles, blocks[out_src], preferred_element_type=jnp.float32
    ).astype(jnp.bfloat16)
    outgoing = jnp.einsum(
        "kt,trd->krd", placing, partials, preferred_element_type=jnp.float32
    ).astype(jnp.bfloat16)
    hub_local = inputs[hub_ids]
    hub_block = jnp.zeros((HUB_PAD, col_count), jnp.bfloat16).at[:hub_count].set(hub_local)
    payload = jnp.concatenate(
        [
            outgoing.reshape(node_count, capacity * tile_side, col_count),
            jnp.broadcast_to(hub_block[None], (node_count, HUB_PAD, col_count)),
        ],
        axis=1,
    )
    arrived = lax.all_to_all(payload, "dom", split_axis=0, concat_axis=0, tiled=True)
    tiles_in = arrived[:, : capacity * tile_side, :].reshape(slot_count, tile_side, col_count)
    hub_rows = arrived[:, capacity * tile_side : capacity * tile_side + hub_count, :].reshape(
        node_count * hub_count, col_count
    )
    from_peers = jnp.einsum(
        "bk,krd->brd", landing, tiles_in, preferred_element_type=jnp.float32
    )
    local_products = jnp.einsum(
        "trs,tsd->trd", local_tiles, blocks[local_cols], preferred_element_type=jnp.float32
    )
    onehot = (local_rows[None, :] == block_ids[:, None]).astype(jnp.float32)
    from_local = jnp.einsum("bt,trd->brd", onehot, local_products, precision=lax.Precision.HIGHEST)
    from_hubs = jnp.dot(hub_adjacency, hub_rows, preferred_element_type=jnp.float32)
    summed = (from_peers + from_local).reshape(vertex_count, col_count) + from_hubs
    return (summed / degree.astype(jnp.float32)[:, None]).astype(jnp.bfloat16)


def per_device(
    features,
    degree,
    hub_ids,
    hub_adjacency,
    local_rows,
    local_cols,
    local_tiles,
    out_dest,
    out_src,
    out_tiles,
    recv_target,
    w_self,
    w_neigh,
    gains,
):
    width = w_self.shape[1]
    tile_side = local_tiles.shape[1]
    placing, landing = routing(
        out_dest, recv_target, features.shape[0] // tile_side, lax.axis_size("dom")
    )
    current = features
    for layer_idx in range(w_self.shape[0]):
        neighbours = aggregate(
            current,
            degree,
            hub_ids,
            hub_adjacency,
            local_rows,
            local_cols,
            local_tiles,
            out_src,
            out_tiles,
            placing,
            landing,
        )
        self_weight = w_self[layer_idx]
        neigh_weight = w_neigh[layer_idx]
        gain_row = gains[layer_idx][None, :]
        own_part = lax.all_gather(current, "feat", axis=1, tiled=True)
        neigh_part = lax.all_gather(neighbours, "feat", axis=1, tiled=True)
        running = jnp.dot(own_part, self_weight, preferred_element_type=jnp.float32)
        mixed = running + jnp.dot(neigh_part, neigh_weight, preferred_element_type=jnp.float32)
        rectified = jnp.maximum(mixed, 0.0)
        squares = lax.psum(jnp.sum(rectified * rectified, axis=1), "feat")
        scaled = (
            gain_row.astype(jnp.float32) * rectified * lax.rsqrt(squares[:, None] / width + EPSILON)
        )
        current = scaled.astype(jnp.bfloat16)
    return current


def solution(mesh):
    in_specs = (
        P("dom", "feat"),
        P("dom"),
        P("dom"),
        P("dom", None),
        P("dom"),
        P("dom"),
        P("dom", None, None),
        P("dom", None),
        P("dom"),
        P("dom", None, None),
        P("dom", None, None),
        P(None, None, "feat"),
        P(None, None, "feat"),
        P(None, "feat"),
    )
    out_specs = P("dom", "feat")
    return jax.shard_map(
        per_device, mesh=mesh, in_specs=in_specs, out_specs=out_specs, check_vma=False
    )
```

```python
import jax
import jax.numpy as jnp
from jax import lax
from jax.sharding import PartitionSpec as P

EPSILON = 1e-06
HUB_PAD = 16


def routing(out_dest, recv_target, block_count, node_count):
    capacity = recv_target.shape[2]
    destination = out_dest[:, 0]
    positions = jnp.arange(destination.shape[0], dtype=jnp.int32)
    matches = (destination[None, :] == destination[:, None]) & (
        positions[None, :] < positions[:, None]
    )
    slot_rank = jnp.sum(matches.astype(jnp.int32), axis=1)
    slots = destination * capacity + slot_rank
    slot_ids = jnp.arange(node_count * capacity, dtype=jnp.int32)
    placing = (slot_ids[:, None] == slots[None, :]).astype(jnp.bfloat16)
    targets = recv_target[0].reshape(-1)
    block_ids = jnp.arange(block_count, dtype=jnp.int32)
    landing = (targets[None, :] == block_ids[:, None]).astype(jnp.bfloat16)
    return placing, landing


def aggregate(
    inputs,
    degree,
    hub_ids,
    hub_adjacency,
    local_rows,
    local_cols,
    local_tiles,
    out_src,
    out_tiles,
    placing,
    landing,
):
    vertex_count, col_count = inputs.shape
    tile_side = local_tiles.shape[1]
    block_count = vertex_count // tile_side
    node_count = lax.axis_size("dom")
    slot_count = placing.shape[0]
    capacity = slot_count // node_count
    hub_count = hub_ids.shape[0]
    blocks = inputs.reshape(block_count, tile_side, col_count)
    block_ids = jnp.arange(block_count, dtype=jnp.int32)
    partials = jnp.einsum(
        "trs,tsd->trd", out_tiles, blocks[out_src], preferred_element_type=jnp.float32
    ).astype(jnp.bfloat16)
    outgoing = jnp.einsum(
        "kt,trd->krd", placing, partials, preferred_element_type=jnp.float32
    ).astype(jnp.bfloat16)
    hub_local = inputs[hub_ids]
    hub_block = jnp.zeros((HUB_PAD, col_count), jnp.bfloat16).at[:hub_count].set(hub_local)
    payload = jnp.concatenate(
        [
            outgoing.reshape(node_count, capacity * tile_side, col_count),
            jnp.broadcast_to(hub_block[None], (node_count, HUB_PAD, col_count)),
        ],
        axis=1,
    )
    arrived = lax.all_to_all(payload, "dom", split_axis=0, concat_axis=0, tiled=True)
    tiles_in = arrived[:, : capacity * tile_side, :].reshape(slot_count, tile_side, col_count)
    hub_rows = arrived[:, capacity * tile_side : capacity * tile_side + hub_count, :].reshape(
        node_count * hub_count, col_count
    )
    from_peers = jnp.einsum(
        "bk,krd->brd", landing, tiles_in, preferred_element_type=jnp.float32
    )
    local_products = jnp.einsum(
        "trs,tsd->trd", local_tiles, blocks[local_cols], preferred_element_type=jnp.float32
    )
    onehot = (local_rows[None, :] == block_ids[:, None]).astype(jnp.float32)
    from_local = jnp.einsum("bt,trd->brd", onehot, local_products, precision=lax.Precision.HIGHEST)
    from_hubs = jnp.dot(hub_adjacency, hub_rows, preferred_element_type=jnp.float32)
    summed = (from_peers + from_local).reshape(vertex_count, col_count) + from_hubs
    return (summed / degree.astype(jnp.float32)[:, None]).astype(jnp.bfloat16)


def feat_to_rows(block):
    feat_count = lax.axis_size("feat")
    row_count, col_count = block.shape
    pieces = block.reshape(feat_count, row_count // feat_count, col_count)
    gathered = lax.all_to_all(pieces, "feat", split_axis=0, concat_axis=0, tiled=True)
    return gathered.transpose(1, 0, 2).reshape(row_count // feat_count, feat_count * col_count)


def rows_to_feat(rows):
    feat_count = lax.axis_size("feat")
    row_count, width = rows.shape
    pieces = rows.reshape(row_count, feat_count, width // feat_count).transpose(1, 0, 2)
    gathered = lax.all_to_all(pieces, "feat", split_axis=0, concat_axis=0, tiled=True)
    return gathered.reshape(feat_count * row_count, width // feat_count)


def mix(own_rows, neigh_rows, self_weight, neigh_weight, gain):
    width = self_weight.shape[1]
    running = jnp.dot(own_rows, self_weight, preferred_element_type=jnp.float32)
    mixed = running + jnp.dot(neigh_rows, neigh_weight, preferred_element_type=jnp.float32)
    rectified = jnp.maximum(mixed, 0.0)
    squares = jnp.sum(rectified * rectified, axis=1, keepdims=True)
    scaled = gain.astype(jnp.float32)[None, :] * rectified * lax.rsqrt(squares / width + EPSILON)
    return scaled.astype(jnp.bfloat16)


def per_device(
    features,
    degree,
    hub_ids,
    hub_adjacency,
    local_rows,
    local_cols,
    local_tiles,
    out_dest,
    out_src,
    out_tiles,
    recv_target,
    w_self,
    w_neigh,
    gains,
):
    tile_side = local_tiles.shape[1]
    placing, landing = routing(
        out_dest, recv_target, features.shape[0] // tile_side, lax.axis_size("dom")
    )
    full_self = lax.all_gather(w_self, "feat", axis=2, tiled=True)
    full_neigh = lax.all_gather(w_neigh, "feat", axis=2, tiled=True)
    full_gains = lax.all_gather(gains, "feat", axis=1, tiled=True)
    current = features
    own_rows = feat_to_rows(features)
    for layer_idx in range(w_self.shape[0]):
        neighbours = aggregate(
            current,
            degree,
            hub_ids,
            hub_adjacency,
            local_rows,
            local_cols,
            local_tiles,
            out_src,
            out_tiles,
            placing,
            landing,
        )
        neigh_rows = feat_to_rows(neighbours)
        own_rows = mix(
            own_rows,
            neigh_rows,
            full_self[layer_idx],
            full_neigh[layer_idx],
            full_gains[layer_idx],
        )
        current = rows_to_feat(own_rows)
    return current


def solution(mesh):
    in_specs = (
        P("dom", "feat"),
        P("dom"),
        P("dom"),
        P("dom", None),
        P("dom"),
        P("dom"),
        P("dom", None, None),
        P("dom", None),
        P("dom"),
        P("dom", None, None),
        P("dom", None, None),
        P(None, None, "feat"),
        P(None, None, "feat"),
        P(None, "feat"),
    )
    out_specs = P("dom", "feat")
    return jax.shard_map(
        per_device, mesh=mesh, in_specs=in_specs, out_specs=out_specs, check_vma=False
    )
```

```python
import jax
import jax.numpy as jnp
from jax import lax
from jax.experimental import pallas as pl
from jax.experimental.pallas import tpu as pltpu
from jax.sharding import PartitionSpec as P

EPSILON = 1e-06
HUB_PAD = 16


def routing(out_dest, recv_target, block_count, node_count):
    capacity = recv_target.shape[2]
    destination = out_dest[:, 0]
    positions = jnp.arange(destination.shape[0], dtype=jnp.int32)
    matches = (destination[None, :] == destination[:, None]) & (
        positions[None, :] < positions[:, None]
    )
    slot_rank = jnp.sum(matches.astype(jnp.int32), axis=1)
    slots = destination * capacity + slot_rank
    targets = recv_target[0].reshape(-1)
    block_ids = jnp.arange(block_count, dtype=jnp.int32)
    landing = (targets[None, :] == block_ids[:, None]).astype(jnp.bfloat16)
    return slots.astype(jnp.int32), landing


def payload_kernel(slot_ref, src_ref, tiles_ref, blocks_ref, hub_ref, out_ref):
    node_count, rows_per_node, _ = out_ref.shape
    tile_count, tile_side, _ = tiles_ref.shape
    tail = rows_per_node - HUB_PAD
    capacity = tail // tile_side
    out_ref[...] = jnp.zeros(out_ref.shape, out_ref.dtype)
    hub = hub_ref[...]

    def put_hub(node, carry):
        out_ref[node, pl.ds(tail, HUB_PAD), :] = hub
        return carry

    lax.fori_loop(0, node_count, put_hub, 0)

    def put_tile(tile, carry):
        slot = slot_ref[tile]
        node = slot // capacity
        first = pl.multiple_of((slot % capacity) * tile_side, tile_side)
        product = jnp.dot(
            tiles_ref[tile], blocks_ref[src_ref[tile]], preferred_element_type=jnp.float32
        )
        out_ref[node, pl.ds(first, tile_side), :] = product.astype(out_ref.dtype)
        return carry

    lax.fori_loop(0, tile_count, put_tile, 0)


def build_payload(slots, sources, tiles, blocks, hub_block, node_count, capacity):
    tile_side = tiles.shape[1]
    col_count = blocks.shape[2]
    rows_per_node = capacity * tile_side + HUB_PAD
    return pl.pallas_call(
        payload_kernel,
        out_shape=jax.ShapeDtypeStruct((node_count, rows_per_node, col_count), blocks.dtype),
        grid_spec=pltpu.PrefetchScalarGridSpec(
            num_scalar_prefetch=2,
            grid=(1,),
            in_specs=[
                pl.BlockSpec(memory_space=pltpu.VMEM),
                pl.BlockSpec(memory_space=pltpu.VMEM),
                pl.BlockSpec(memory_space=pltpu.VMEM),
            ],
            out_specs=pl.BlockSpec(memory_space=pltpu.VMEM),
        ),
    )(slots, sources, tiles, blocks, hub_block)


def aggregate(
    inputs,
    degree,
    hub_ids,
    hub_adjacency,
    local_rows,
    local_cols,
    local_tiles,
    out_src,
    out_tiles,
    slots,
    landing,
    anchor,
):
    vertex_count, col_count = inputs.shape
    tile_side = local_tiles.shape[1]
    block_count = vertex_count // tile_side
    node_count = lax.axis_size("dom")
    slot_count = landing.shape[1]
    capacity = slot_count // node_count
    hub_count = hub_ids.shape[0]
    blocks = inputs.reshape(block_count, tile_side, col_count)
    block_ids = jnp.arange(block_count, dtype=jnp.int32)
    hub_local = inputs[hub_ids]
    hub_block = jnp.zeros((HUB_PAD, col_count), jnp.bfloat16).at[:hub_count].set(hub_local)
    payload = build_payload(
        slots, out_src.astype(jnp.int32), out_tiles, blocks, hub_block, node_count, capacity
    )
    if anchor is not None:
        payload, anchor = lax.optimization_barrier((payload, anchor))
    arrived = lax.all_to_all(payload, "dom", split_axis=0, concat_axis=0, tiled=True)
    tiles_in = arrived[:, : capacity * tile_side, :].reshape(slot_count, tile_side, col_count)
    hub_rows = arrived[:, capacity * tile_side : capacity * tile_side + hub_count, :].reshape(
        node_count * hub_count, col_count
    )
    from_peers = jnp.einsum(
        "bk,krd->brd", landing, tiles_in, preferred_element_type=jnp.float32
    )
    local_products = jnp.einsum(
        "trs,tsd->trd", local_tiles, blocks[local_cols], preferred_element_type=jnp.float32
    )
    onehot = (local_rows[None, :] == block_ids[:, None]).astype(jnp.float32)
    from_local = jnp.einsum("bt,trd->brd", onehot, local_products, precision=lax.Precision.HIGHEST)
    from_hubs = jnp.dot(hub_adjacency, hub_rows, preferred_element_type=jnp.float32)
    summed = (from_peers + from_local).reshape(vertex_count, col_count) + from_hubs
    return (summed / degree.astype(jnp.float32)[:, None]).astype(jnp.bfloat16), anchor


def feat_to_rows(block):
    feat_count = lax.axis_size("feat")
    row_count, col_count = block.shape
    pieces = block.reshape(feat_count, row_count // feat_count, col_count)
    gathered = lax.all_to_all(pieces, "feat", split_axis=0, concat_axis=0, tiled=True)
    return gathered.transpose(1, 0, 2).reshape(row_count // feat_count, feat_count * col_count)


def rows_to_feat(rows):
    feat_count = lax.axis_size("feat")
    row_count, width = rows.shape
    pieces = rows.reshape(row_count, feat_count, width // feat_count).transpose(1, 0, 2)
    gathered = lax.all_to_all(pieces, "feat", split_axis=0, concat_axis=0, tiled=True)
    return gathered.reshape(feat_count * row_count, width // feat_count)


def mix(own_rows, neigh_rows, self_weight, neigh_weight, gain):
    width = self_weight.shape[1]
    running = jnp.dot(own_rows, self_weight, preferred_element_type=jnp.float32)
    mixed = running + jnp.dot(neigh_rows, neigh_weight, preferred_element_type=jnp.float32)
    rectified = jnp.maximum(mixed, 0.0)
    squares = jnp.sum(rectified * rectified, axis=1, keepdims=True)
    scaled = gain.astype(jnp.float32)[None, :] * rectified * lax.rsqrt(squares / width + EPSILON)
    return scaled.astype(jnp.bfloat16)


def per_device(
    features,
    degree,
    hub_ids,
    hub_adjacency,
    local_rows,
    local_cols,
    local_tiles,
    out_dest,
    out_src,
    out_tiles,
    recv_target,
    w_self,
    w_neigh,
    gains,
):
    tile_side = local_tiles.shape[1]
    slots, landing = routing(
        out_dest, recv_target, features.shape[0] // tile_side, lax.axis_size("dom")
    )
    full_self = lax.all_gather(w_self, "feat", axis=2, tiled=True)
    full_neigh = lax.all_gather(w_neigh, "feat", axis=2, tiled=True)
    full_gains = lax.all_gather(gains, "feat", axis=1, tiled=True)
    current = features
    own_rows = feat_to_rows(features)
    for layer_idx in range(w_self.shape[0]):
        neighbours, anchored = aggregate(
            current,
            degree,
            hub_ids,
            hub_adjacency,
            local_rows,
            local_cols,
            local_tiles,
            out_src,
            out_tiles,
            slots,
            landing,
            own_rows if layer_idx == 0 else None,
        )
        if anchored is not None:
            own_rows = anchored
        neigh_rows = feat_to_rows(neighbours)
        own_rows = mix(
            own_rows,
            neigh_rows,
            full_self[layer_idx],
            full_neigh[layer_idx],
            full_gains[layer_idx],
        )
        current = rows_to_feat(own_rows)
    return current


def solution(mesh):
    in_specs = (
        P("dom", "feat"),
        P("dom"),
        P("dom"),
        P("dom", None),
        P("dom"),
        P("dom"),
        P("dom", None, None),
        P("dom", None),
        P("dom"),
        P("dom", None, None),
        P("dom", None, None),
        P(None, None, "feat"),
        P(None, None, "feat"),
        P(None, "feat"),
    )
    out_specs = P("dom", "feat")
    return jax.shard_map(
        per_device, mesh=mesh, in_specs=in_specs, out_specs=out_specs, check_vma=False
    )
```

```python
import jax
import jax.numpy as jnp
from jax import lax
from jax.experimental import pallas as pl
from jax.experimental.pallas import tpu as pltpu
from jax.sharding import PartitionSpec as P

EPSILON = 1e-06
HUB_PAD = 16


def routing(out_dest, recv_target, block_count, node_count):
    capacity = recv_target.shape[2]
    destination = out_dest[:, 0]
    positions = jnp.arange(destination.shape[0], dtype=jnp.int32)
    matches = (destination[None, :] == destination[:, None]) & (
        positions[None, :] < positions[:, None]
    )
    slot_rank = jnp.sum(matches.astype(jnp.int32), axis=1)
    slots = destination * capacity + slot_rank
    targets = recv_target[0].reshape(-1)
    block_ids = jnp.arange(block_count, dtype=jnp.int32)
    landing = (targets[None, :] == block_ids[:, None]).astype(jnp.bfloat16)
    return slots.astype(jnp.int32), landing


def payload_kernel(slot_ref, src_ref, tiles_ref, blocks_ref, hub_ref, out_ref):
    node_count, rows_per_node, _ = out_ref.shape
    tile_count, tile_side, _ = tiles_ref.shape
    tail = rows_per_node - HUB_PAD
    capacity = tail // tile_side
    out_ref[...] = jnp.zeros(out_ref.shape, out_ref.dtype)
    hub = hub_ref[...]

    def put_hub(node, carry):
        out_ref[node, pl.ds(tail, HUB_PAD), :] = hub
        return carry

    lax.fori_loop(0, node_count, put_hub, 0, unroll=8)

    def put_tile(tile, carry):
        slot = slot_ref[tile]
        node = slot // capacity
        first = pl.multiple_of((slot % capacity) * tile_side, tile_side)
        product = jnp.dot(
            tiles_ref[tile], blocks_ref[src_ref[tile]], preferred_element_type=jnp.float32
        )
        out_ref[node, pl.ds(first, tile_side), :] = product.astype(out_ref.dtype)
        return carry

    lax.fori_loop(0, tile_count, put_tile, 0, unroll=8)


def build_payload(slots, sources, tiles, blocks, hub_block, node_count, capacity):
    tile_side = tiles.shape[1]
    col_count = blocks.shape[2]
    rows_per_node = capacity * tile_side + HUB_PAD
    return pl.pallas_call(
        payload_kernel,
        out_shape=jax.ShapeDtypeStruct((node_count, rows_per_node, col_count), blocks.dtype),
        grid_spec=pltpu.PrefetchScalarGridSpec(
            num_scalar_prefetch=2,
            grid=(1,),
            in_specs=[
                pl.BlockSpec(memory_space=pltpu.VMEM),
                pl.BlockSpec(memory_space=pltpu.VMEM),
                pl.BlockSpec(memory_space=pltpu.VMEM),
            ],
            out_specs=pl.BlockSpec(memory_space=pltpu.VMEM),
        ),
    )(slots, sources, tiles, blocks, hub_block)


def aggregate(
    inputs,
    degree,
    hub_ids,
    hub_adjacency,
    local_rows,
    local_cols,
    local_tiles,
    out_src,
    out_tiles,
    slots,
    landing,
    anchor,
):
    vertex_count, col_count = inputs.shape
    tile_side = local_tiles.shape[1]
    block_count = vertex_count // tile_side
    node_count = lax.axis_size("dom")
    slot_count = landing.shape[1]
    capacity = slot_count // node_count
    hub_count = hub_ids.shape[0]
    blocks = inputs.reshape(block_count, tile_side, col_count)
    block_ids = jnp.arange(block_count, dtype=jnp.int32)
    hub_local = inputs[hub_ids]
    hub_block = jnp.zeros((HUB_PAD, col_count), jnp.bfloat16).at[:hub_count].set(hub_local)
    payload = build_payload(
        slots, out_src.astype(jnp.int32), out_tiles, blocks, hub_block, node_count, capacity
    )
    if anchor is not None:
        payload, anchor = lax.optimization_barrier((payload, anchor))
    arrived = lax.all_to_all(payload, "dom", split_axis=0, concat_axis=0, tiled=True)
    tiles_in = arrived[:, : capacity * tile_side, :].reshape(slot_count, tile_side, col_count)
    hub_rows = arrived[:, capacity * tile_side : capacity * tile_side + hub_count, :].reshape(
        node_count * hub_count, col_count
    )
    from_peers = jnp.einsum(
        "bk,krd->brd", landing, tiles_in, preferred_element_type=jnp.float32
    )
    local_products = jnp.einsum(
        "trs,tsd->trd", local_tiles, blocks[local_cols], preferred_element_type=jnp.float32
    )
    onehot = (local_rows[None, :] == block_ids[:, None]).astype(jnp.float32)
    from_local = jnp.einsum("bt,trd->brd", onehot, local_products, precision=lax.Precision.HIGHEST)
    from_hubs = jnp.dot(hub_adjacency, hub_rows, preferred_element_type=jnp.float32)
    summed = (from_peers + from_local).reshape(vertex_count, col_count) + from_hubs
    return (summed / degree.astype(jnp.float32)[:, None]).astype(jnp.bfloat16), anchor


def feat_to_rows(block):
    feat_count = lax.axis_size("feat")
    row_count, col_count = block.shape
    pieces = block.reshape(feat_count, row_count // feat_count, col_count)
    gathered = lax.all_to_all(pieces, "feat", split_axis=0, concat_axis=0, tiled=True)
    return gathered.transpose(1, 0, 2).reshape(row_count // feat_count, feat_count * col_count)


def rows_to_feat(rows):
    feat_count = lax.axis_size("feat")
    row_count, width = rows.shape
    pieces = rows.reshape(row_count, feat_count, width // feat_count).transpose(1, 0, 2)
    gathered = lax.all_to_all(pieces, "feat", split_axis=0, concat_axis=0, tiled=True)
    return gathered.reshape(feat_count * row_count, width // feat_count)


def mix(own_rows, neigh_rows, self_weight, neigh_weight, gain):
    width = self_weight.shape[1]
    running = jnp.dot(own_rows, self_weight, preferred_element_type=jnp.float32)
    mixed = running + jnp.dot(neigh_rows, neigh_weight, preferred_element_type=jnp.float32)
    rectified = jnp.maximum(mixed, 0.0)
    squares = jnp.sum(rectified * rectified, axis=1, keepdims=True)
    scaled = gain.astype(jnp.float32)[None, :] * rectified * lax.rsqrt(squares / width + EPSILON)
    return scaled.astype(jnp.bfloat16)


def per_device(
    features,
    degree,
    hub_ids,
    hub_adjacency,
    local_rows,
    local_cols,
    local_tiles,
    out_dest,
    out_src,
    out_tiles,
    recv_target,
    w_self,
    w_neigh,
    gains,
):
    tile_side = local_tiles.shape[1]
    slots, landing = routing(
        out_dest, recv_target, features.shape[0] // tile_side, lax.axis_size("dom")
    )
    full_self = lax.all_gather(w_self, "feat", axis=2, tiled=True)
    full_neigh = lax.all_gather(w_neigh, "feat", axis=2, tiled=True)
    full_gains = lax.all_gather(gains, "feat", axis=1, tiled=True)
    current = features
    own_rows = feat_to_rows(features)
    for layer_idx in range(w_self.shape[0]):
        neighbours, anchored = aggregate(
            current,
            degree,
            hub_ids,
            hub_adjacency,
            local_rows,
            local_cols,
            local_tiles,
            out_src,
            out_tiles,
            slots,
            landing,
            own_rows if layer_idx == 0 else None,
        )
        if anchored is not None:
            own_rows = anchored
        neigh_rows = feat_to_rows(neighbours)
        own_rows = mix(
            own_rows,
            neigh_rows,
            full_self[layer_idx],
            full_neigh[layer_idx],
            full_gains[layer_idx],
        )
        current = rows_to_feat(own_rows)
    return current


def solution(mesh):
    in_specs = (
        P("dom", "feat"),
        P("dom"),
        P("dom"),
        P("dom", None),
        P("dom"),
        P("dom"),
        P("dom", None, None),
        P("dom", None),
        P("dom"),
        P("dom", None, None),
        P("dom", None, None),
        P(None, None, "feat"),
        P(None, None, "feat"),
        P(None, "feat"),
    )
    out_specs = P("dom", "feat")
    return jax.shard_map(
        per_device, mesh=mesh, in_specs=in_specs, out_specs=out_specs, check_vma=False
    )
```

```python
import jax
import jax.numpy as jnp
from jax import lax
from jax.experimental import pallas as pl
from jax.experimental.pallas import tpu as pltpu
from jax.sharding import PartitionSpec as P

EPSILON = 1e-06
HUB_PAD = 16


def routing(out_dest, recv_target, block_count, node_count):
    capacity = recv_target.shape[2]
    destination = out_dest[:, 0]
    positions = jnp.arange(destination.shape[0], dtype=jnp.int32)
    matches = (destination[None, :] == destination[:, None]) & (
        positions[None, :] < positions[:, None]
    )
    slot_rank = jnp.sum(matches.astype(jnp.int32), axis=1)
    slots = destination * capacity + slot_rank
    targets = recv_target[0].reshape(-1)
    block_ids = jnp.arange(block_count, dtype=jnp.int32)
    landing = (targets[None, :] == block_ids[:, None]).astype(jnp.bfloat16)
    return slots.astype(jnp.int32), landing


def payload_kernel(slot_ref, src_ref, tiles_ref, blocks_ref, hub_ref, out_ref):
    node_count, rows_per_node, _ = out_ref.shape
    tile_count, tile_side, _ = tiles_ref.shape
    tail = rows_per_node - HUB_PAD
    capacity = tail // tile_side
    out_ref[...] = jnp.zeros(out_ref.shape, out_ref.dtype)
    hub = hub_ref[...]

    def put_hub(node, carry):
        out_ref[node, pl.ds(tail, HUB_PAD), :] = hub
        return carry

    lax.fori_loop(0, node_count, put_hub, 0, unroll=8)

    def put_tile(tile, carry):
        slot = slot_ref[tile]
        node = slot // capacity
        first = pl.multiple_of((slot % capacity) * tile_side, tile_side)
        product = jnp.dot(
            tiles_ref[tile], blocks_ref[src_ref[tile]], preferred_element_type=jnp.float32
        )
        out_ref[node, pl.ds(first, tile_side), :] = product.astype(out_ref.dtype)
        return carry

    lax.fori_loop(0, tile_count, put_tile, 0, unroll=8)


def build_payload(slots, sources, tiles, blocks, hub_block, node_count, capacity):
    tile_side = tiles.shape[1]
    col_count = blocks.shape[2]
    rows_per_node = capacity * tile_side + HUB_PAD
    return pl.pallas_call(
        payload_kernel,
        out_shape=jax.ShapeDtypeStruct((node_count, rows_per_node, col_count), blocks.dtype),
        grid_spec=pltpu.PrefetchScalarGridSpec(
            num_scalar_prefetch=2,
            grid=(1,),
            in_specs=[
                pl.BlockSpec(memory_space=pltpu.VMEM),
                pl.BlockSpec(memory_space=pltpu.VMEM),
                pl.BlockSpec(memory_space=pltpu.VMEM),
            ],
            out_specs=pl.BlockSpec(memory_space=pltpu.VMEM),
        ),
    )(slots, sources, tiles, blocks, hub_block)


def aggregate(
    inputs,
    degree,
    hub_ids,
    hub_adjacency,
    local_rows,
    local_cols,
    local_tiles,
    out_src,
    out_tiles,
    slots,
    landing,
    anchor,
):
    vertex_count, col_count = inputs.shape
    tile_side = local_tiles.shape[1]
    block_count = vertex_count // tile_side
    node_count = lax.axis_size("dom")
    slot_count = landing.shape[1]
    capacity = slot_count // node_count
    hub_count = hub_ids.shape[0]
    blocks = inputs.reshape(block_count, tile_side, col_count)
    block_ids = jnp.arange(block_count, dtype=jnp.int32)
    hub_local = inputs[hub_ids]
    hub_block = jnp.zeros((HUB_PAD, col_count), jnp.bfloat16).at[:hub_count].set(hub_local)
    payload = build_payload(
        slots, out_src.astype(jnp.int32), out_tiles, blocks, hub_block, node_count, capacity
    )
    if anchor is not None:
        payload, anchor = lax.optimization_barrier((payload, anchor))
    arrived = lax.all_to_all(payload, "dom", split_axis=0, concat_axis=0, tiled=True)
    tiles_in = arrived[:, : capacity * tile_side, :].reshape(slot_count, tile_side, col_count)
    hub_rows = arrived[:, capacity * tile_side : capacity * tile_side + hub_count, :].reshape(
        node_count * hub_count, col_count
    )
    from_peers = jnp.einsum(
        "bk,krd->brd", landing, tiles_in, preferred_element_type=jnp.float32
    )
    local_products = jnp.einsum(
        "trs,tsd->trd", local_tiles, blocks[local_cols], preferred_element_type=jnp.float32
    )
    onehot = (local_rows[None, :] == block_ids[:, None]).astype(jnp.float32)
    from_local = jnp.einsum("bt,trd->brd", onehot, local_products, precision=lax.Precision.HIGHEST)
    from_hubs = jnp.dot(hub_adjacency, hub_rows, preferred_element_type=jnp.float32)
    summed = (from_peers + from_local).reshape(vertex_count, col_count) + from_hubs
    return (summed / degree.astype(jnp.float32)[:, None]).astype(jnp.bfloat16), anchor


def feat_to_rows(block):
    feat_count = lax.axis_size("feat")
    row_count, col_count = block.shape
    pieces = block.reshape(feat_count, row_count // feat_count, col_count)
    gathered = lax.all_to_all(pieces, "feat", split_axis=0, concat_axis=0, tiled=True)
    return gathered.transpose(1, 0, 2).reshape(row_count // feat_count, feat_count * col_count)


def rows_to_feat(rows):
    feat_count = lax.axis_size("feat")
    row_count, width = rows.shape
    pieces = rows.reshape(row_count, feat_count, width // feat_count).transpose(1, 0, 2)
    gathered = lax.all_to_all(pieces, "feat", split_axis=0, concat_axis=0, tiled=True)
    return gathered.reshape(feat_count * row_count, width // feat_count)


def mix(own_rows, neigh_rows, self_weight, neigh_weight, gain):
    width = self_weight.shape[1]
    running = jnp.dot(own_rows, self_weight, preferred_element_type=jnp.float32)
    mixed = running + jnp.dot(neigh_rows, neigh_weight, preferred_element_type=jnp.float32)
    rectified = jnp.maximum(mixed, 0.0)
    squares = jnp.sum(rectified * rectified, axis=1, keepdims=True)
    scaled = gain.astype(jnp.float32)[None, :] * rectified * lax.rsqrt(squares / width + EPSILON)
    return scaled.astype(jnp.bfloat16)


def gather_weights(w_self, w_neigh, gains):
    feat_count = lax.axis_size("feat")
    layer_count, depth, slice_width = w_self.shape
    gain_rows = jnp.zeros((layer_count, HUB_PAD, slice_width), gains.dtype).at[:, 0, :].set(gains)
    stacked = jnp.concatenate([w_self, w_neigh, gain_rows], axis=1)
    own = lax.axis_index("feat")
    pieces = [stacked]
    for shift in range(1, feat_count):
        pairs = [(source, (source + shift) % feat_count) for source in range(feat_count)]
        pieces.append(lax.ppermute(stacked, "feat", pairs))
    received = jnp.stack(pieces)
    order = (own - jnp.arange(feat_count, dtype=jnp.int32)) % feat_count
    ordered = jnp.take(received, jnp.argsort(order), axis=0)
    full = ordered.transpose(1, 2, 0, 3).reshape(layer_count, stacked.shape[1], feat_count * slice_width)
    return full[:, :depth], full[:, depth : 2 * depth], full[:, 2 * depth]


def per_device(
    features,
    degree,
    hub_ids,
    hub_adjacency,
    local_rows,
    local_cols,
    local_tiles,
    out_dest,
    out_src,
    out_tiles,
    recv_target,
    w_self,
    w_neigh,
    gains,
):
    tile_side = local_tiles.shape[1]
    slots, landing = routing(
        out_dest, recv_target, features.shape[0] // tile_side, lax.axis_size("dom")
    )
    full_self, full_neigh, full_gains = gather_weights(w_self, w_neigh, gains)
    current = features
    own_rows = feat_to_rows(features)
    for layer_idx in range(w_self.shape[0]):
        neighbours, anchored = aggregate(
            current,
            degree,
            hub_ids,
            hub_adjacency,
            local_rows,
            local_cols,
            local_tiles,
            out_src,
            out_tiles,
            slots,
            landing,
            own_rows if layer_idx == 0 else None,
        )
        if anchored is not None:
            own_rows = anchored
        neigh_rows = feat_to_rows(neighbours)
        own_rows = mix(
            own_rows,
            neigh_rows,
            full_self[layer_idx],
            full_neigh[layer_idx],
            full_gains[layer_idx],
        )
        current = rows_to_feat(own_rows)
    return current


def solution(mesh):
    in_specs = (
        P("dom", "feat"),
        P("dom"),
        P("dom"),
        P("dom", None),
        P("dom"),
        P("dom"),
        P("dom", None, None),
        P("dom", None),
        P("dom"),
        P("dom", None, None),
        P("dom", None, None),
        P(None, None, "feat"),
        P(None, None, "feat"),
        P(None, "feat"),
    )
    out_specs = P("dom", "feat")
    return jax.shard_map(
        per_device, mesh=mesh, in_specs=in_specs, out_specs=out_specs, check_vma=False
    )
```

```python
import jax
import jax.numpy as jnp
from jax import lax
from jax.experimental import pallas as pl
from jax.experimental.pallas import tpu as pltpu
from jax.sharding import PartitionSpec as P

EPSILON = 1e-06
HUB_PAD = 16


def routing(out_dest, recv_target, block_count, node_count):
    capacity = recv_target.shape[2]
    destination = out_dest[:, 0]
    positions = jnp.arange(destination.shape[0], dtype=jnp.int32)
    matches = (destination[None, :] == destination[:, None]) & (
        positions[None, :] < positions[:, None]
    )
    slot_rank = jnp.sum(matches.astype(jnp.int32), axis=1)
    slots = destination * capacity + slot_rank
    targets = recv_target[0].reshape(-1)
    block_ids = jnp.arange(block_count, dtype=jnp.int32)
    landing = (targets[None, :] == block_ids[:, None]).astype(jnp.bfloat16)
    return slots.astype(jnp.int32), landing


def payload_kernel(slot_ref, src_ref, tiles_ref, blocks_ref, hub_ref, out_ref):
    node_count, rows_per_node, _ = out_ref.shape
    tile_count, tile_side, _ = tiles_ref.shape
    tail = rows_per_node - HUB_PAD
    capacity = tail // tile_side
    out_ref[...] = jnp.zeros(out_ref.shape, out_ref.dtype)
    hub = hub_ref[...]

    def put_hub(node, carry):
        out_ref[node, pl.ds(tail, HUB_PAD), :] = hub
        return carry

    lax.fori_loop(0, node_count, put_hub, 0, unroll=8)

    def put_tile(tile, carry):
        slot = slot_ref[tile]
        node = slot // capacity
        first = pl.multiple_of((slot % capacity) * tile_side, tile_side)
        product = jnp.dot(
            tiles_ref[tile], blocks_ref[src_ref[tile]], preferred_element_type=jnp.float32
        )
        out_ref[node, pl.ds(first, tile_side), :] = product.astype(out_ref.dtype)
        return carry

    lax.fori_loop(0, tile_count, put_tile, 0, unroll=8)


def build_payload(slots, sources, tiles, blocks, hub_block, node_count, capacity):
    tile_side = tiles.shape[1]
    col_count = blocks.shape[2]
    rows_per_node = capacity * tile_side + HUB_PAD
    return pl.pallas_call(
        payload_kernel,
        out_shape=jax.ShapeDtypeStruct((node_count, rows_per_node, col_count), blocks.dtype),
        grid_spec=pltpu.PrefetchScalarGridSpec(
            num_scalar_prefetch=2,
            grid=(1,),
            in_specs=[
                pl.BlockSpec(memory_space=pltpu.VMEM),
                pl.BlockSpec(memory_space=pltpu.VMEM),
                pl.BlockSpec(memory_space=pltpu.VMEM),
            ],
            out_specs=pl.BlockSpec(memory_space=pltpu.VMEM),
        ),
    )(slots, sources, tiles, blocks, hub_block)


def aggregate(
    inputs,
    degree,
    hub_ids,
    hub_adjacency,
    local_rows,
    local_cols,
    local_tiles,
    out_src,
    out_tiles,
    slots,
    landing,
    anchor,
):
    vertex_count, col_count = inputs.shape
    tile_side = local_tiles.shape[1]
    block_count = vertex_count // tile_side
    node_count = lax.axis_size("dom")
    slot_count = landing.shape[1]
    capacity = slot_count // node_count
    hub_count = hub_ids.shape[0]
    blocks = inputs.reshape(block_count, tile_side, col_count)
    block_ids = jnp.arange(block_count, dtype=jnp.int32)
    hub_local = inputs[hub_ids]
    hub_block = jnp.zeros((HUB_PAD, col_count), jnp.bfloat16).at[:hub_count].set(hub_local)
    payload = build_payload(
        slots, out_src.astype(jnp.int32), out_tiles, blocks, hub_block, node_count, capacity
    )
    if anchor is not None:
        payload, anchor = lax.optimization_barrier((payload, anchor))
    arrived = lax.all_to_all(payload, "dom", split_axis=0, concat_axis=0, tiled=True)
    tiles_in = arrived[:, : capacity * tile_side, :].reshape(slot_count, tile_side, col_count)
    hub_rows = arrived[:, capacity * tile_side : capacity * tile_side + hub_count, :].reshape(
        node_count * hub_count, col_count
    )
    from_peers = jnp.einsum(
        "bk,krd->brd", landing, tiles_in, preferred_element_type=jnp.float32
    )
    local_products = jnp.einsum(
        "trs,tsd->trd", local_tiles, blocks[local_cols], preferred_element_type=jnp.float32
    )
    onehot = (local_rows[None, :] == block_ids[:, None]).astype(jnp.float32)
    from_local = jnp.einsum("bt,trd->brd", onehot, local_products, precision=lax.Precision.HIGHEST)
    from_hubs = jnp.dot(hub_adjacency, hub_rows, preferred_element_type=jnp.float32)
    summed = (from_peers + from_local).reshape(vertex_count, col_count) + from_hubs
    return (summed / degree.astype(jnp.float32)[:, None]).astype(jnp.bfloat16), anchor


def feat_to_rows(block):
    feat_count = lax.axis_size("feat")
    row_count, col_count = block.shape
    pieces = block.reshape(feat_count, row_count // feat_count, col_count)
    gathered = lax.all_to_all(pieces, "feat", split_axis=0, concat_axis=0, tiled=True)
    return gathered.transpose(1, 0, 2).reshape(row_count // feat_count, feat_count * col_count)


def rows_to_feat(rows):
    feat_count = lax.axis_size("feat")
    row_count, width = rows.shape
    pieces = rows.reshape(row_count, feat_count, width // feat_count).transpose(1, 0, 2)
    gathered = lax.all_to_all(pieces, "feat", split_axis=0, concat_axis=0, tiled=True)
    return gathered.reshape(feat_count * row_count, width // feat_count)


def mix(own_rows, neigh_rows, self_weight, neigh_weight, gain):
    width = self_weight.shape[1]
    running = jnp.dot(own_rows, self_weight, preferred_element_type=jnp.float32)
    mixed = running + jnp.dot(neigh_rows, neigh_weight, preferred_element_type=jnp.float32)
    rectified = jnp.maximum(mixed, 0.0)
    squares = jnp.sum(rectified * rectified, axis=1, keepdims=True)
    scaled = gain.astype(jnp.float32)[None, :] * rectified * lax.rsqrt(squares / width + EPSILON)
    return scaled.astype(jnp.bfloat16)


def gather_weights(w_self, w_neigh, gains):
    feat_count = lax.axis_size("feat")
    layer_count, depth, slice_width = w_self.shape
    gain_rows = jnp.zeros((layer_count, HUB_PAD, slice_width), gains.dtype).at[:, 0, :].set(gains)
    stacked = jnp.concatenate([w_self, w_neigh, gain_rows], axis=1)
    pieces = [stacked]
    for shift in range(1, feat_count):
        pairs = [(source, (source + shift) % feat_count) for source in range(feat_count)]
        pieces.append(lax.ppermute(stacked, "feat", pairs))
    full = jnp.concatenate(pieces, axis=2)
    return full[:, :depth], full[:, depth : 2 * depth], full[:, 2 * depth]


def natural_columns(shifted):
    feat_count = lax.axis_size("feat")
    row_count, width = shifted.shape
    order = (lax.axis_index("feat") - jnp.arange(feat_count, dtype=jnp.int32)) % feat_count
    blocks = shifted.reshape(row_count, feat_count, width // feat_count)
    return jnp.take(blocks, order, axis=1).reshape(row_count, width)


def per_device(
    features,
    degree,
    hub_ids,
    hub_adjacency,
    local_rows,
    local_cols,
    local_tiles,
    out_dest,
    out_src,
    out_tiles,
    recv_target,
    w_self,
    w_neigh,
    gains,
):
    tile_side = local_tiles.shape[1]
    slots, landing = routing(
        out_dest, recv_target, features.shape[0] // tile_side, lax.axis_size("dom")
    )
    full_self, full_neigh, full_gains = gather_weights(w_self, w_neigh, gains)
    current = features
    own_rows = feat_to_rows(features)
    for layer_idx in range(w_self.shape[0]):
        neighbours, anchored = aggregate(
            current,
            degree,
            hub_ids,
            hub_adjacency,
            local_rows,
            local_cols,
            local_tiles,
            out_src,
            out_tiles,
            slots,
            landing,
            own_rows if layer_idx == 0 else None,
        )
        if anchored is not None:
            own_rows = anchored
        neigh_rows = feat_to_rows(neighbours)
        own_rows = natural_columns(
            mix(
                own_rows,
                neigh_rows,
                full_self[layer_idx],
                full_neigh[layer_idx],
                full_gains[layer_idx],
            )
        )
        current = rows_to_feat(own_rows)
    return current


def solution(mesh):
    in_specs = (
        P("dom", "feat"),
        P("dom"),
        P("dom"),
        P("dom", None),
        P("dom"),
        P("dom"),
        P("dom", None, None),
        P("dom", None),
        P("dom"),
        P("dom", None, None),
        P("dom", None, None),
        P(None, None, "feat"),
        P(None, None, "feat"),
        P(None, "feat"),
    )
    out_specs = P("dom", "feat")
    return jax.shard_map(
        per_device, mesh=mesh, in_specs=in_specs, out_specs=out_specs, check_vma=False
    )
```

```python
import jax
import jax.numpy as jnp
from jax import lax
from jax.experimental import pallas as pl
from jax.experimental.pallas import tpu as pltpu
from jax.sharding import PartitionSpec as P

EPSILON = 1e-06
HUB_PAD = 16


def routing(out_dest, recv_target, block_count, node_count):
    targets = recv_target[0].reshape(-1)
    block_ids = jnp.arange(block_count, dtype=jnp.int32)
    landing = (targets[None, :] == block_ids[:, None]).astype(jnp.bfloat16)
    return out_dest[:, 0].astype(jnp.int32), landing


def payload_kernel(dest_ref, src_ref, hub_ref, tiles_ref, blocks_ref, out_ref, counts_ref):
    node_count, rows_per_node, col_count = out_ref.shape
    tile_count, tile_side, _ = tiles_ref.shape
    tail = rows_per_node - HUB_PAD
    capacity = tail // tile_side
    out_ref[...] = jnp.zeros(out_ref.shape, out_ref.dtype)

    def clear(node, carry):
        counts_ref[node] = 0
        return carry

    lax.fori_loop(0, node_count, clear, 0, unroll=8)
    lanes = lax.broadcasted_iota(jnp.int32, (HUB_PAD, col_count), 0)
    hub = jnp.zeros((HUB_PAD, col_count), jnp.float32)
    for index in range(hub_ref.shape[0]):
        vertex = hub_ref[index]
        block = vertex // tile_side
        row = vertex % tile_side
        start = pl.multiple_of((row // HUB_PAD) * HUB_PAD, HUB_PAD)
        window = blocks_ref[block, pl.ds(start, HUB_PAD), :].astype(jnp.float32)
        picked = jnp.sum(jnp.where(lanes == row % HUB_PAD, window, 0.0), axis=0, keepdims=True)
        hub = jnp.where(lanes == index, picked, hub)
    hub = hub.astype(out_ref.dtype)

    def put_hub(node, carry):
        out_ref[node, pl.ds(tail, HUB_PAD), :] = hub
        return carry

    lax.fori_loop(0, node_count, put_hub, 0, unroll=8)

    def put_tile(tile, carry):
        node = dest_ref[tile]
        rank = counts_ref[node]
        counts_ref[node] = rank + 1
        first = pl.multiple_of(jnp.minimum(rank, capacity - 1) * tile_side, tile_side)
        product = jnp.dot(
            tiles_ref[tile], blocks_ref[src_ref[tile]], preferred_element_type=jnp.float32
        )
        out_ref[node, pl.ds(first, tile_side), :] = product.astype(out_ref.dtype)
        return carry

    lax.fori_loop(0, tile_count, put_tile, 0, unroll=8)


def build_payload(destination, sources, hubs, tiles, blocks, node_count, capacity):
    tile_side = tiles.shape[1]
    col_count = blocks.shape[2]
    rows_per_node = capacity * tile_side + HUB_PAD
    return pl.pallas_call(
        payload_kernel,
        out_shape=jax.ShapeDtypeStruct((node_count, rows_per_node, col_count), blocks.dtype),
        grid_spec=pltpu.PrefetchScalarGridSpec(
            num_scalar_prefetch=3,
            grid=(1,),
            in_specs=[
                pl.BlockSpec(memory_space=pltpu.VMEM),
                pl.BlockSpec(memory_space=pltpu.VMEM),
            ],
            out_specs=pl.BlockSpec(memory_space=pltpu.VMEM),
            scratch_shapes=[pltpu.SMEM((node_count,), jnp.int32)],
        ),
    )(destination, sources, hubs, tiles, blocks)


def aggregate(
    inputs,
    degree,
    hub_ids,
    hub_adjacency,
    local_rows,
    local_cols,
    local_tiles,
    out_src,
    out_tiles,
    destination,
    landing,
    anchor,
):
    vertex_count, col_count = inputs.shape
    tile_side = local_tiles.shape[1]
    block_count = vertex_count // tile_side
    node_count = lax.axis_size("dom")
    slot_count = landing.shape[1]
    capacity = slot_count // node_count
    hub_count = hub_ids.shape[0]
    blocks = inputs.reshape(block_count, tile_side, col_count)
    block_ids = jnp.arange(block_count, dtype=jnp.int32)
    payload = build_payload(
        destination, out_src.astype(jnp.int32), hub_ids.astype(jnp.int32), out_tiles, blocks,
        node_count, capacity,
    )
    if anchor is not None:
        payload, anchor = lax.optimization_barrier((payload, anchor))
    arrived = lax.all_to_all(payload, "dom", split_axis=0, concat_axis=0, tiled=True)
    tiles_in = arrived[:, : capacity * tile_side, :].reshape(slot_count, tile_side, col_count)
    hub_rows = arrived[:, capacity * tile_side : capacity * tile_side + hub_count, :].reshape(
        node_count * hub_count, col_count
    )
    from_peers = jnp.einsum(
        "bk,krd->brd", landing, tiles_in, preferred_element_type=jnp.float32
    )
    local_products = jnp.einsum(
        "trs,tsd->trd", local_tiles, blocks[local_cols], preferred_element_type=jnp.float32
    )
    onehot = (local_rows[None, :] == block_ids[:, None]).astype(jnp.float32)
    from_local = jnp.einsum("bt,trd->brd", onehot, local_products, precision=lax.Precision.HIGHEST)
    from_hubs = jnp.dot(hub_adjacency, hub_rows, preferred_element_type=jnp.float32)
    summed = (from_peers + from_local).reshape(vertex_count, col_count) + from_hubs
    return (summed / degree.astype(jnp.float32)[:, None]).astype(jnp.bfloat16), anchor


def feat_to_rows(block):
    feat_count = lax.axis_size("feat")
    row_count, col_count = block.shape
    pieces = block.reshape(feat_count, row_count // feat_count, col_count)
    gathered = lax.all_to_all(pieces, "feat", split_axis=0, concat_axis=0, tiled=True)
    return gathered.transpose(1, 0, 2).reshape(row_count // feat_count, feat_count * col_count)


def rows_to_feat(rows):
    feat_count = lax.axis_size("feat")
    row_count, width = rows.shape
    pieces = rows.reshape(row_count, feat_count, width // feat_count).transpose(1, 0, 2)
    gathered = lax.all_to_all(pieces, "feat", split_axis=0, concat_axis=0, tiled=True)
    return gathered.reshape(feat_count * row_count, width // feat_count)


def mix(own_rows, neigh_rows, self_weight, neigh_weight, gain):
    width = self_weight.shape[1]
    running = jnp.dot(own_rows, self_weight, preferred_element_type=jnp.float32)
    mixed = running + jnp.dot(neigh_rows, neigh_weight, preferred_element_type=jnp.float32)
    rectified = jnp.maximum(mixed, 0.0)
    squares = jnp.sum(rectified * rectified, axis=1, keepdims=True)
    scaled = gain.astype(jnp.float32)[None, :] * rectified * lax.rsqrt(squares / width + EPSILON)
    return scaled.astype(jnp.bfloat16)


def gather_weights(w_self, w_neigh, gains):
    feat_count = lax.axis_size("feat")
    layer_count, depth, slice_width = w_self.shape
    gain_rows = jnp.zeros((layer_count, HUB_PAD, slice_width), gains.dtype).at[:, 0, :].set(gains)
    stacked = jnp.concatenate([w_self, w_neigh, gain_rows], axis=1)
    pieces = [stacked]
    for shift in range(1, feat_count):
        pairs = [(source, (source + shift) % feat_count) for source in range(feat_count)]
        pieces.append(lax.ppermute(stacked, "feat", pairs))
    full = jnp.concatenate(pieces, axis=2)
    return full[:, :depth], full[:, depth : 2 * depth], full[:, 2 * depth]


def natural_columns(shifted):
    feat_count = lax.axis_size("feat")
    row_count, width = shifted.shape
    order = (lax.axis_index("feat") - jnp.arange(feat_count, dtype=jnp.int32)) % feat_count
    blocks = shifted.reshape(row_count, feat_count, width // feat_count)
    return jnp.take(blocks, order, axis=1).reshape(row_count, width)


def per_device(
    features,
    degree,
    hub_ids,
    hub_adjacency,
    local_rows,
    local_cols,
    local_tiles,
    out_dest,
    out_src,
    out_tiles,
    recv_target,
    w_self,
    w_neigh,
    gains,
):
    tile_side = local_tiles.shape[1]
    destination, landing = routing(
        out_dest, recv_target, features.shape[0] // tile_side, lax.axis_size("dom")
    )
    full_self, full_neigh, full_gains = gather_weights(w_self, w_neigh, gains)
    current = features
    own_rows = feat_to_rows(features)
    for layer_idx in range(w_self.shape[0]):
        neighbours, anchored = aggregate(
            current,
            degree,
            hub_ids,
            hub_adjacency,
            local_rows,
            local_cols,
            local_tiles,
            out_src,
            out_tiles,
            destination,
            landing,
            own_rows if layer_idx == 0 else None,
        )
        if anchored is not None:
            own_rows = anchored
        neigh_rows = feat_to_rows(neighbours)
        own_rows = natural_columns(
            mix(
                own_rows,
                neigh_rows,
                full_self[layer_idx],
                full_neigh[layer_idx],
                full_gains[layer_idx],
            )
        )
        current = rows_to_feat(own_rows)
    return current


def solution(mesh):
    in_specs = (
        P("dom", "feat"),
        P("dom"),
        P("dom"),
        P("dom", None),
        P("dom"),
        P("dom"),
        P("dom", None, None),
        P("dom", None),
        P("dom"),
        P("dom", None, None),
        P("dom", None, None),
        P(None, None, "feat"),
        P(None, None, "feat"),
        P(None, "feat"),
    )
    out_specs = P("dom", "feat")
    return jax.shard_map(
        per_device, mesh=mesh, in_specs=in_specs, out_specs=out_specs, check_vma=False
    )
```

```python
import jax
import jax.numpy as jnp
from jax import lax
from jax.experimental import pallas as pl
from jax.experimental.pallas import tpu as pltpu
from jax.sharding import PartitionSpec as P

EPSILON = 1e-06
HUB_PAD = 16


def routing(out_dest, recv_target, block_count, node_count):
    targets = recv_target[0].reshape(-1)
    block_ids = jnp.arange(block_count, dtype=jnp.int32)
    landing = (targets[None, :] == block_ids[:, None]).astype(jnp.bfloat16)
    return out_dest[:, 0].astype(jnp.int32), landing


def payload_kernel(dest_ref, src_ref, hub_ref, tiles_ref, blocks_ref, out_ref, counts_ref):
    node_count, rows_per_node, col_count = out_ref.shape
    tile_count, tile_side, _ = tiles_ref.shape
    tail = rows_per_node - HUB_PAD
    capacity = tail // tile_side
    out_ref[...] = jnp.zeros(out_ref.shape, out_ref.dtype)

    def clear(node, carry):
        counts_ref[node] = 0
        return carry

    lax.fori_loop(0, node_count, clear, 0, unroll=8)
    lanes = lax.broadcasted_iota(jnp.int32, (HUB_PAD, col_count), 0)
    hub = jnp.zeros((HUB_PAD, col_count), jnp.float32)
    for index in range(hub_ref.shape[0]):
        vertex = hub_ref[index]
        block = vertex // tile_side
        row = vertex % tile_side
        start = pl.multiple_of((row // HUB_PAD) * HUB_PAD, HUB_PAD)
        window = blocks_ref[block, pl.ds(start, HUB_PAD), :].astype(jnp.float32)
        picked = jnp.sum(jnp.where(lanes == row % HUB_PAD, window, 0.0), axis=0, keepdims=True)
        hub = jnp.where(lanes == index, picked, hub)
    hub = hub.astype(out_ref.dtype)

    def put_hub(node, carry):
        out_ref[node, pl.ds(tail, HUB_PAD), :] = hub
        return carry

    lax.fori_loop(0, node_count, put_hub, 0, unroll=8)

    def put_tile(tile, carry):
        node = dest_ref[tile]
        rank = counts_ref[node]
        counts_ref[node] = rank + 1
        first = pl.multiple_of(jnp.minimum(rank, capacity - 1) * tile_side, tile_side)
        product = jnp.dot(
            tiles_ref[tile], blocks_ref[src_ref[tile]], preferred_element_type=jnp.float32
        )
        out_ref[node, pl.ds(first, tile_side), :] = product.astype(out_ref.dtype)
        return carry

    lax.fori_loop(0, tile_count, put_tile, 0, unroll=8)


def build_payload(destination, sources, hubs, tiles, blocks, node_count, capacity):
    tile_side = tiles.shape[1]
    col_count = blocks.shape[2]
    rows_per_node = capacity * tile_side + HUB_PAD
    return pl.pallas_call(
        payload_kernel,
        out_shape=jax.ShapeDtypeStruct((node_count, rows_per_node, col_count), blocks.dtype),
        grid_spec=pltpu.PrefetchScalarGridSpec(
            num_scalar_prefetch=3,
            grid=(1,),
            in_specs=[
                pl.BlockSpec(memory_space=pltpu.VMEM),
                pl.BlockSpec(memory_space=pltpu.VMEM),
            ],
            out_specs=pl.BlockSpec(memory_space=pltpu.VMEM),
            scratch_shapes=[pltpu.SMEM((node_count,), jnp.int32)],
        ),
    )(destination, sources, hubs, tiles, blocks)


def aggregate(
    inputs,
    degree,
    hub_ids,
    hub_adjacency,
    local_rows,
    local_cols,
    local_tiles,
    out_src,
    out_tiles,
    destination,
    landing,
    anchor,
):
    vertex_count, col_count = inputs.shape
    tile_side = local_tiles.shape[1]
    block_count = vertex_count // tile_side
    node_count = lax.axis_size("dom")
    slot_count = landing.shape[1]
    capacity = slot_count // node_count
    hub_count = hub_ids.shape[0]
    blocks = inputs.reshape(block_count, tile_side, col_count)
    block_ids = jnp.arange(block_count, dtype=jnp.int32)
    payload = build_payload(
        destination, out_src.astype(jnp.int32), hub_ids.astype(jnp.int32), out_tiles, blocks,
        node_count, capacity,
    )
    if anchor is not None:
        payload, anchor = lax.optimization_barrier((payload, anchor))
    arrived = lax.all_to_all(payload, "dom", split_axis=0, concat_axis=0, tiled=True)
    tiles_in = arrived[:, : capacity * tile_side, :].reshape(slot_count, tile_side, col_count)
    hub_rows = arrived[:, capacity * tile_side : capacity * tile_side + hub_count, :].reshape(
        node_count * hub_count, col_count
    )
    from_peers = jnp.einsum(
        "bk,krd->brd", landing, tiles_in, preferred_element_type=jnp.float32
    )
    local_products = jnp.einsum(
        "trs,tsd->trd", local_tiles, blocks[local_cols], preferred_element_type=jnp.float32
    )
    onehot = (local_rows[None, :] == block_ids[:, None]).astype(jnp.float32)
    from_local = jnp.einsum("bt,trd->brd", onehot, local_products, precision=lax.Precision.HIGHEST)
    from_hubs = jnp.dot(hub_adjacency, hub_rows, preferred_element_type=jnp.float32)
    summed = (from_peers + from_local).reshape(vertex_count, col_count) + from_hubs
    return (summed / degree.astype(jnp.float32)[:, None]).astype(jnp.bfloat16), anchor


def feat_to_rows(block):
    feat_count = lax.axis_size("feat")
    row_count, col_count = block.shape
    pieces = block.reshape(feat_count, row_count // feat_count, col_count)
    gathered = lax.all_to_all(pieces, "feat", split_axis=0, concat_axis=0, tiled=True)
    return gathered.transpose(1, 0, 2).reshape(row_count // feat_count, feat_count * col_count)


def rows_to_feat(rows):
    feat_count = lax.axis_size("feat")
    row_count, width = rows.shape
    pieces = rows.reshape(row_count, feat_count, width // feat_count).transpose(1, 0, 2)
    gathered = lax.all_to_all(pieces, "feat", split_axis=0, concat_axis=0, tiled=True)
    return gathered.reshape(feat_count * row_count, width // feat_count)


def mix(own_rows, neigh_rows, self_weight, neigh_weight, gain):
    width = self_weight.shape[1]
    running = jnp.dot(own_rows, self_weight, preferred_element_type=jnp.float32)
    mixed = running + jnp.dot(neigh_rows, neigh_weight, preferred_element_type=jnp.float32)
    rectified = jnp.maximum(mixed, 0.0)
    squares = jnp.sum(rectified * rectified, axis=1, keepdims=True)
    scaled = gain.astype(jnp.float32)[None, :] * rectified * lax.rsqrt(squares / width + EPSILON)
    return scaled.astype(jnp.bfloat16)


def gather_weights(w_self, w_neigh, gains):
    feat_count = lax.axis_size("feat")
    layer_count, depth, slice_width = w_self.shape
    gain_rows = jnp.zeros((layer_count, HUB_PAD, slice_width), gains.dtype).at[:, 0, :].set(gains)
    stacked = jnp.concatenate([w_self, w_neigh, gain_rows], axis=1)
    pieces = [stacked]
    for shift in range(1, feat_count):
        pairs = [(source, (source + shift) % feat_count) for source in range(feat_count)]
        pieces.append(lax.ppermute(stacked, "feat", pairs))
    full = jnp.concatenate(pieces, axis=2)
    return full[:, :depth], full[:, depth : 2 * depth], full[:, 2 * depth]


def natural_columns(shifted):
    feat_count = lax.axis_size("feat")
    row_count, width = shifted.shape
    order = (lax.axis_index("feat") - jnp.arange(feat_count, dtype=jnp.int32)) % feat_count
    blocks = shifted.reshape(row_count, feat_count, width // feat_count)
    return jnp.take(blocks, order, axis=1).reshape(row_count, width)


def feat_to_rows_by_permutes(block):
    feat_count = lax.axis_size("feat")
    row_count, col_count = block.shape
    own = lax.axis_index("feat")
    chunks = block.reshape(feat_count, row_count // feat_count, col_count)
    pieces = [chunks[own]]
    for shift in range(1, feat_count):
        pairs = [(source, (source + shift) % feat_count) for source in range(feat_count)]
        pieces.append(lax.ppermute(chunks[(own + shift) % feat_count], "feat", pairs))
    return natural_columns(jnp.concatenate(pieces, axis=1))


def per_device(
    features,
    degree,
    hub_ids,
    hub_adjacency,
    local_rows,
    local_cols,
    local_tiles,
    out_dest,
    out_src,
    out_tiles,
    recv_target,
    w_self,
    w_neigh,
    gains,
):
    tile_side = local_tiles.shape[1]
    destination, landing = routing(
        out_dest, recv_target, features.shape[0] // tile_side, lax.axis_size("dom")
    )
    full_self, full_neigh, full_gains = gather_weights(w_self, w_neigh, gains)
    current = features
    own_rows = feat_to_rows_by_permutes(features)
    for layer_idx in range(w_self.shape[0]):
        neighbours, anchored = aggregate(
            current,
            degree,
            hub_ids,
            hub_adjacency,
            local_rows,
            local_cols,
            local_tiles,
            out_src,
            out_tiles,
            destination,
            landing,
            None,
        )
        if anchored is not None:
            own_rows = anchored
        neigh_rows = feat_to_rows(neighbours)
        own_rows = natural_columns(
            mix(
                own_rows,
                neigh_rows,
                full_self[layer_idx],
                full_neigh[layer_idx],
                full_gains[layer_idx],
            )
        )
        current = rows_to_feat(own_rows)
    return current


def solution(mesh):
    in_specs = (
        P("dom", "feat"),
        P("dom"),
        P("dom"),
        P("dom", None),
        P("dom"),
        P("dom"),
        P("dom", None, None),
        P("dom", None),
        P("dom"),
        P("dom", None, None),
        P("dom", None, None),
        P(None, None, "feat"),
        P(None, None, "feat"),
        P(None, "feat"),
    )
    out_specs = P("dom", "feat")
    return jax.shard_map(
        per_device, mesh=mesh, in_specs=in_specs, out_specs=out_specs, check_vma=False
    )
```

```python
import jax
import jax.numpy as jnp
from jax import lax
from jax.experimental import pallas as pl
from jax.experimental.pallas import tpu as pltpu
from jax.sharding import PartitionSpec as P

EPSILON = 1e-06
HUB_PAD = 8
WINDOW = 16


def routing(out_dest, recv_target, block_count, node_count):
    targets = recv_target[0].reshape(-1)
    block_ids = jnp.arange(block_count, dtype=jnp.int32)
    landing = (targets[None, :] == block_ids[:, None]).astype(jnp.bfloat16)
    return out_dest[:, 0].astype(jnp.int32), landing


def payload_kernel(dest_ref, src_ref, hub_ref, tiles_ref, blocks_ref, out_ref, counts_ref):
    node_count, rows_per_node, col_count = out_ref.shape
    tile_count, tile_side, _ = tiles_ref.shape
    tail = rows_per_node - HUB_PAD
    capacity = tail // tile_side
    out_ref[...] = jnp.zeros(out_ref.shape, out_ref.dtype)

    def clear(node, carry):
        counts_ref[node] = 0
        return carry

    lax.fori_loop(0, node_count, clear, 0, unroll=8)
    window_rows = lax.broadcasted_iota(jnp.int32, (WINDOW, col_count), 0)
    lanes = lax.broadcasted_iota(jnp.int32, (HUB_PAD, col_count), 0)
    hub = jnp.zeros((HUB_PAD, col_count), jnp.float32)
    for index in range(hub_ref.shape[0]):
        vertex = hub_ref[index]
        block = vertex // tile_side
        row = vertex % tile_side
        start = pl.multiple_of((row // WINDOW) * WINDOW, WINDOW)
        window = blocks_ref[block, pl.ds(start, WINDOW), :].astype(jnp.float32)
        picked = jnp.sum(jnp.where(window_rows == row % WINDOW, window, 0.0), axis=0, keepdims=True)
        hub = jnp.where(lanes == index, picked, hub)
    hub = hub.astype(out_ref.dtype)

    def put_hub(node, carry):
        out_ref[node, pl.ds(tail, HUB_PAD), :] = hub
        return carry

    lax.fori_loop(0, node_count, put_hub, 0, unroll=8)

    def put_tile(tile, carry):
        node = dest_ref[tile]
        rank = counts_ref[node]
        counts_ref[node] = rank + 1
        first = pl.multiple_of(jnp.minimum(rank, capacity - 1) * tile_side, tile_side)
        product = jnp.dot(
            tiles_ref[tile], blocks_ref[src_ref[tile]], preferred_element_type=jnp.float32
        )
        out_ref[node, pl.ds(first, tile_side), :] = product.astype(out_ref.dtype)
        return carry

    lax.fori_loop(0, tile_count, put_tile, 0, unroll=8)


def build_payload(destination, sources, hubs, tiles, blocks, node_count, capacity):
    tile_side = tiles.shape[1]
    col_count = blocks.shape[2]
    rows_per_node = capacity * tile_side + HUB_PAD
    return pl.pallas_call(
        payload_kernel,
        out_shape=jax.ShapeDtypeStruct((node_count, rows_per_node, col_count), blocks.dtype),
        grid_spec=pltpu.PrefetchScalarGridSpec(
            num_scalar_prefetch=3,
            grid=(1,),
            in_specs=[
                pl.BlockSpec(memory_space=pltpu.VMEM),
                pl.BlockSpec(memory_space=pltpu.VMEM),
            ],
            out_specs=pl.BlockSpec(memory_space=pltpu.VMEM),
            scratch_shapes=[pltpu.SMEM((node_count,), jnp.int32)],
        ),
    )(destination, sources, hubs, tiles, blocks)


def aggregate(
    inputs,
    degree,
    hub_ids,
    hub_adjacency,
    local_rows,
    local_cols,
    local_tiles,
    out_src,
    out_tiles,
    destination,
    landing,
    anchor,
):
    vertex_count, col_count = inputs.shape
    tile_side = local_tiles.shape[1]
    block_count = vertex_count // tile_side
    node_count = lax.axis_size("dom")
    slot_count = landing.shape[1]
    capacity = slot_count // node_count
    hub_count = hub_ids.shape[0]
    blocks = inputs.reshape(block_count, tile_side, col_count)
    block_ids = jnp.arange(block_count, dtype=jnp.int32)
    payload = build_payload(
        destination, out_src.astype(jnp.int32), hub_ids.astype(jnp.int32), out_tiles, blocks,
        node_count, capacity,
    )
    if anchor is not None:
        payload, anchor = lax.optimization_barrier((payload, anchor))
    arrived = lax.all_to_all(payload, "dom", split_axis=0, concat_axis=0, tiled=True)
    tiles_in = arrived[:, : capacity * tile_side, :].reshape(slot_count, tile_side, col_count)
    hub_rows = arrived[:, capacity * tile_side : capacity * tile_side + hub_count, :].reshape(
        node_count * hub_count, col_count
    )
    from_peers = jnp.einsum(
        "bk,krd->brd", landing, tiles_in, preferred_element_type=jnp.float32
    )
    local_products = jnp.einsum(
        "trs,tsd->trd", local_tiles, blocks[local_cols], preferred_element_type=jnp.float32
    )
    onehot = (local_rows[None, :] == block_ids[:, None]).astype(jnp.float32)
    from_local = jnp.einsum("bt,trd->brd", onehot, local_products, precision=lax.Precision.HIGHEST)
    from_hubs = jnp.dot(hub_adjacency, hub_rows, preferred_element_type=jnp.float32)
    summed = (from_peers + from_local).reshape(vertex_count, col_count) + from_hubs
    return (summed / degree.astype(jnp.float32)[:, None]).astype(jnp.bfloat16), anchor


def feat_to_rows(block):
    feat_count = lax.axis_size("feat")
    row_count, col_count = block.shape
    pieces = block.reshape(feat_count, row_count // feat_count, col_count)
    gathered = lax.all_to_all(pieces, "feat", split_axis=0, concat_axis=0, tiled=True)
    return gathered.transpose(1, 0, 2).reshape(row_count // feat_count, feat_count * col_count)


def rows_to_feat(rows):
    feat_count = lax.axis_size("feat")
    row_count, width = rows.shape
    pieces = rows.reshape(row_count, feat_count, width // feat_count).transpose(1, 0, 2)
    gathered = lax.all_to_all(pieces, "feat", split_axis=0, concat_axis=0, tiled=True)
    return gathered.reshape(feat_count * row_count, width // feat_count)


def mix(own_rows, neigh_rows, self_weight, neigh_weight, gain):
    width = self_weight.shape[1]
    running = jnp.dot(own_rows, self_weight, preferred_element_type=jnp.float32)
    mixed = running + jnp.dot(neigh_rows, neigh_weight, preferred_element_type=jnp.float32)
    rectified = jnp.maximum(mixed, 0.0)
    squares = jnp.sum(rectified * rectified, axis=1, keepdims=True)
    scaled = gain.astype(jnp.float32)[None, :] * rectified * lax.rsqrt(squares / width + EPSILON)
    return scaled.astype(jnp.bfloat16)


def gather_weights(w_self, w_neigh, gains):
    feat_count = lax.axis_size("feat")
    layer_count, depth, slice_width = w_self.shape
    gain_rows = jnp.zeros((layer_count, HUB_PAD, slice_width), gains.dtype).at[:, 0, :].set(gains)
    stacked = jnp.concatenate([w_self, w_neigh, gain_rows], axis=1)
    pieces = [stacked]
    for shift in range(1, feat_count):
        pairs = [(source, (source + shift) % feat_count) for source in range(feat_count)]
        pieces.append(lax.ppermute(stacked, "feat", pairs))
    full = jnp.concatenate(pieces, axis=2)
    return full[:, :depth], full[:, depth : 2 * depth], full[:, 2 * depth]


def natural_columns(shifted):
    feat_count = lax.axis_size("feat")
    row_count, width = shifted.shape
    order = (lax.axis_index("feat") - jnp.arange(feat_count, dtype=jnp.int32)) % feat_count
    blocks = shifted.reshape(row_count, feat_count, width // feat_count)
    return jnp.take(blocks, order, axis=1).reshape(row_count, width)


def per_device(
    features,
    degree,
    hub_ids,
    hub_adjacency,
    local_rows,
    local_cols,
    local_tiles,
    out_dest,
    out_src,
    out_tiles,
    recv_target,
    w_self,
    w_neigh,
    gains,
):
    tile_side = local_tiles.shape[1]
    destination, landing = routing(
        out_dest, recv_target, features.shape[0] // tile_side, lax.axis_size("dom")
    )
    full_self, full_neigh, full_gains = gather_weights(w_self, w_neigh, gains)
    current = features
    own_rows = feat_to_rows(features)
    for layer_idx in range(w_self.shape[0]):
        neighbours, anchored = aggregate(
            current,
            degree,
            hub_ids,
            hub_adjacency,
            local_rows,
            local_cols,
            local_tiles,
            out_src,
            out_tiles,
            destination,
            landing,
            own_rows if layer_idx == 0 else None,
        )
        if anchored is not None:
            own_rows = anchored
        neigh_rows = feat_to_rows(neighbours)
        own_rows = natural_columns(
            mix(
                own_rows,
                neigh_rows,
                full_self[layer_idx],
                full_neigh[layer_idx],
                full_gains[layer_idx],
            )
        )
        current = rows_to_feat(own_rows)
    return current


def solution(mesh):
    in_specs = (
        P("dom", "feat"),
        P("dom"),
        P("dom"),
        P("dom", None),
        P("dom"),
        P("dom"),
        P("dom", None, None),
        P("dom", None),
        P("dom"),
        P("dom", None, None),
        P("dom", None, None),
        P(None, None, "feat"),
        P(None, None, "feat"),
        P(None, "feat"),
    )
    out_specs = P("dom", "feat")
    return jax.shard_map(
        per_device, mesh=mesh, in_specs=in_specs, out_specs=out_specs, check_vma=False
    )
```

```python
import jax
import jax.numpy as jnp
from jax import lax
from jax.experimental import pallas as pl
from jax.experimental.pallas import tpu as pltpu
from jax.sharding import PartitionSpec as P

EPSILON = 1e-06
HUB_PAD = 8
WINDOW = 16


def routing(out_dest, recv_target, block_count, node_count):
    targets = recv_target[0].reshape(-1)
    block_ids = jnp.arange(block_count, dtype=jnp.int32)
    landing = (targets[None, :] == block_ids[:, None]).astype(jnp.bfloat16)
    return out_dest[:, 0].astype(jnp.int32), landing


def payload_kernel(dest_ref, src_ref, hub_ref, tiles_ref, blocks_ref, out_ref, counts_ref):
    node_count, rows_per_node, col_count = out_ref.shape
    tile_count, tile_side, _ = tiles_ref.shape
    tail = rows_per_node - HUB_PAD
    capacity = tail // tile_side
    out_ref[...] = jnp.zeros(out_ref.shape, out_ref.dtype)

    def clear(node, carry):
        counts_ref[node] = 0
        return carry

    lax.fori_loop(0, node_count, clear, 0, unroll=8)
    window_rows = lax.broadcasted_iota(jnp.int32, (WINDOW, col_count), 0)
    lanes = lax.broadcasted_iota(jnp.int32, (HUB_PAD, col_count), 0)
    hub = jnp.zeros((HUB_PAD, col_count), jnp.float32)
    for index in range(hub_ref.shape[0]):
        vertex = hub_ref[index]
        block = vertex // tile_side
        row = vertex % tile_side
        start = pl.multiple_of((row // WINDOW) * WINDOW, WINDOW)
        window = blocks_ref[block, pl.ds(start, WINDOW), :].astype(jnp.float32)
        picked = jnp.sum(jnp.where(window_rows == row % WINDOW, window, 0.0), axis=0, keepdims=True)
        hub = jnp.where(lanes == index, picked, hub)
    hub = hub.astype(out_ref.dtype)

    def put_hub(node, carry):
        out_ref[node, pl.ds(tail, HUB_PAD), :] = hub
        return carry

    lax.fori_loop(0, node_count, put_hub, 0, unroll=8)

    def put_tile(tile, carry):
        node = dest_ref[tile]
        rank = counts_ref[node]
        counts_ref[node] = rank + 1
        first = pl.multiple_of(jnp.minimum(rank, capacity - 1) * tile_side, tile_side)
        product = jnp.dot(
            tiles_ref[tile], blocks_ref[src_ref[tile]], preferred_element_type=jnp.float32
        )
        out_ref[node, pl.ds(first, tile_side), :] = product.astype(out_ref.dtype)
        return carry

    lax.fori_loop(0, tile_count, put_tile, 0, unroll=True)


def build_payload(destination, sources, hubs, tiles, blocks, node_count, capacity):
    tile_side = tiles.shape[1]
    col_count = blocks.shape[2]
    rows_per_node = capacity * tile_side + HUB_PAD
    return pl.pallas_call(
        payload_kernel,
        out_shape=jax.ShapeDtypeStruct((node_count, rows_per_node, col_count), blocks.dtype),
        grid_spec=pltpu.PrefetchScalarGridSpec(
            num_scalar_prefetch=3,
            grid=(1,),
            in_specs=[
                pl.BlockSpec(memory_space=pltpu.VMEM),
                pl.BlockSpec(memory_space=pltpu.VMEM),
            ],
            out_specs=pl.BlockSpec(memory_space=pltpu.VMEM),
            scratch_shapes=[pltpu.SMEM((node_count,), jnp.int32)],
        ),
    )(destination, sources, hubs, tiles, blocks)


def aggregate(
    inputs,
    degree,
    hub_ids,
    hub_adjacency,
    local_rows,
    local_cols,
    local_tiles,
    out_src,
    out_tiles,
    destination,
    landing,
    anchor,
):
    vertex_count, col_count = inputs.shape
    tile_side = local_tiles.shape[1]
    block_count = vertex_count // tile_side
    node_count = lax.axis_size("dom")
    slot_count = landing.shape[1]
    capacity = slot_count // node_count
    hub_count = hub_ids.shape[0]
    blocks = inputs.reshape(block_count, tile_side, col_count)
    block_ids = jnp.arange(block_count, dtype=jnp.int32)
    payload = build_payload(
        destination, out_src.astype(jnp.int32), hub_ids.astype(jnp.int32), out_tiles, blocks,
        node_count, capacity,
    )
    if anchor is not None:
        payload, anchor = lax.optimization_barrier((payload, anchor))
    arrived = lax.all_to_all(payload, "dom", split_axis=0, concat_axis=0, tiled=True)
    tiles_in = arrived[:, : capacity * tile_side, :].reshape(slot_count, tile_side, col_count)
    hub_rows = arrived[:, capacity * tile_side : capacity * tile_side + hub_count, :].reshape(
        node_count * hub_count, col_count
    )
    from_peers = jnp.einsum(
        "bk,krd->brd", landing, tiles_in, preferred_element_type=jnp.float32
    )
    local_products = jnp.einsum(
        "trs,tsd->trd", local_tiles, blocks[local_cols], preferred_element_type=jnp.float32
    )
    onehot = (local_rows[None, :] == block_ids[:, None]).astype(jnp.float32)
    from_local = jnp.einsum("bt,trd->brd", onehot, local_products, precision=lax.Precision.HIGHEST)
    from_hubs = jnp.dot(hub_adjacency, hub_rows, preferred_element_type=jnp.float32)
    summed = (from_peers + from_local).reshape(vertex_count, col_count) + from_hubs
    return (summed / degree.astype(jnp.float32)[:, None]).astype(jnp.bfloat16), anchor


def feat_to_rows(block):
    feat_count = lax.axis_size("feat")
    row_count, col_count = block.shape
    pieces = block.reshape(feat_count, row_count // feat_count, col_count)
    gathered = lax.all_to_all(pieces, "feat", split_axis=0, concat_axis=0, tiled=True)
    return gathered.transpose(1, 0, 2).reshape(row_count // feat_count, feat_count * col_count)


def rows_to_feat(rows):
    feat_count = lax.axis_size("feat")
    row_count, width = rows.shape
    pieces = rows.reshape(row_count, feat_count, width // feat_count).transpose(1, 0, 2)
    gathered = lax.all_to_all(pieces, "feat", split_axis=0, concat_axis=0, tiled=True)
    return gathered.reshape(feat_count * row_count, width // feat_count)


def mix(own_rows, neigh_rows, self_weight, neigh_weight, gain):
    width = self_weight.shape[1]
    running = jnp.dot(own_rows, self_weight, preferred_element_type=jnp.float32)
    mixed = running + jnp.dot(neigh_rows, neigh_weight, preferred_element_type=jnp.float32)
    rectified = jnp.maximum(mixed, 0.0)
    squares = jnp.sum(rectified * rectified, axis=1, keepdims=True)
    scaled = gain.astype(jnp.float32)[None, :] * rectified * lax.rsqrt(squares / width + EPSILON)
    return scaled.astype(jnp.bfloat16)


def gather_weights(w_self, w_neigh, gains):
    feat_count = lax.axis_size("feat")
    layer_count, depth, slice_width = w_self.shape
    gain_rows = jnp.zeros((layer_count, HUB_PAD, slice_width), gains.dtype).at[:, 0, :].set(gains)
    stacked = jnp.concatenate([w_self, w_neigh, gain_rows], axis=1)
    pieces = [stacked]
    for shift in range(1, feat_count):
        pairs = [(source, (source + shift) % feat_count) for source in range(feat_count)]
        pieces.append(lax.ppermute(stacked, "feat", pairs))
    full = jnp.concatenate(pieces, axis=2)
    return full[:, :depth], full[:, depth : 2 * depth], full[:, 2 * depth]


def natural_columns(shifted):
    feat_count = lax.axis_size("feat")
    row_count, width = shifted.shape
    order = (lax.axis_index("feat") - jnp.arange(feat_count, dtype=jnp.int32)) % feat_count
    blocks = shifted.reshape(row_count, feat_count, width // feat_count)
    return jnp.take(blocks, order, axis=1).reshape(row_count, width)


def per_device(
    features,
    degree,
    hub_ids,
    hub_adjacency,
    local_rows,
    local_cols,
    local_tiles,
    out_dest,
    out_src,
    out_tiles,
    recv_target,
    w_self,
    w_neigh,
    gains,
):
    tile_side = local_tiles.shape[1]
    destination, landing = routing(
        out_dest, recv_target, features.shape[0] // tile_side, lax.axis_size("dom")
    )
    full_self, full_neigh, full_gains = gather_weights(w_self, w_neigh, gains)
    current = features
    own_rows = feat_to_rows(features)
    for layer_idx in range(w_self.shape[0]):
        neighbours, anchored = aggregate(
            current,
            degree,
            hub_ids,
            hub_adjacency,
            local_rows,
            local_cols,
            local_tiles,
            out_src,
            out_tiles,
            destination,
            landing,
            own_rows if layer_idx == 0 else None,
        )
        if anchored is not None:
            own_rows = anchored
        neigh_rows = feat_to_rows(neighbours)
        own_rows = natural_columns(
            mix(
                own_rows,
                neigh_rows,
                full_self[layer_idx],
                full_neigh[layer_idx],
                full_gains[layer_idx],
            )
        )
        current = rows_to_feat(own_rows)
    return current


def solution(mesh):
    in_specs = (
        P("dom", "feat"),
        P("dom"),
        P("dom"),
        P("dom", None),
        P("dom"),
        P("dom"),
        P("dom", None, None),
        P("dom", None),
        P("dom"),
        P("dom", None, None),
        P("dom", None, None),
        P(None, None, "feat"),
        P(None, None, "feat"),
        P(None, "feat"),
    )
    out_specs = P("dom", "feat")
    return jax.shard_map(
        per_device, mesh=mesh, in_specs=in_specs, out_specs=out_specs, check_vma=False
    )
```

```python
import jax
import jax.numpy as jnp
from jax import lax
from jax.experimental import pallas as pl
from jax.experimental.pallas import tpu as pltpu
from jax.sharding import PartitionSpec as P

EPSILON = 1e-06
HUB_PAD = 8
WINDOW = 16


def routing(out_dest, recv_target, block_count, node_count):
    targets = recv_target[0].reshape(-1)
    block_ids = jnp.arange(block_count, dtype=jnp.int32)
    landing = (targets[None, :] == block_ids[:, None]).astype(jnp.bfloat16)
    return out_dest[:, 0].astype(jnp.int32), landing


def payload_kernel(dest_ref, src_ref, hub_ref, tiles_ref, blocks_ref, out_ref, hub_out_ref, counts_ref):
    node_count, rows_per_node, col_count = out_ref.shape
    tile_count, tile_side, _ = tiles_ref.shape
    capacity = rows_per_node // tile_side
    out_ref[...] = jnp.zeros(out_ref.shape, out_ref.dtype)

    def clear(node, carry):
        counts_ref[node] = 0
        return carry

    lax.fori_loop(0, node_count, clear, 0, unroll=8)
    window_rows = lax.broadcasted_iota(jnp.int32, (WINDOW, col_count), 0)
    lanes = lax.broadcasted_iota(jnp.int32, (HUB_PAD, col_count), 0)
    hub = jnp.zeros((HUB_PAD, col_count), jnp.float32)
    for index in range(hub_ref.shape[0]):
        vertex = hub_ref[index]
        block = vertex // tile_side
        row = vertex % tile_side
        start = pl.multiple_of((row // WINDOW) * WINDOW, WINDOW)
        window = blocks_ref[block, pl.ds(start, WINDOW), :].astype(jnp.float32)
        picked = jnp.sum(jnp.where(window_rows == row % WINDOW, window, 0.0), axis=0, keepdims=True)
        hub = jnp.where(lanes == index, picked, hub)
    hub = hub.astype(out_ref.dtype)

    def put_hub(node, carry):
        hub_out_ref[node] = hub
        return carry

    lax.fori_loop(0, node_count, put_hub, 0, unroll=8)

    def put_tile(tile, carry):
        node = dest_ref[tile]
        rank = counts_ref[node]
        counts_ref[node] = rank + 1
        first = pl.multiple_of(jnp.minimum(rank, capacity - 1) * tile_side, tile_side)
        product = jnp.dot(
            tiles_ref[tile], blocks_ref[src_ref[tile]], preferred_element_type=jnp.float32
        )
        out_ref[node, pl.ds(first, tile_side), :] = product.astype(out_ref.dtype)
        return carry

    lax.fori_loop(0, tile_count, put_tile, 0, unroll=8)


def build_payload(destination, sources, hubs, tiles, blocks, node_count, capacity):
    tile_side = tiles.shape[1]
    col_count = blocks.shape[2]
    rows_per_node = capacity * tile_side
    return pl.pallas_call(
        payload_kernel,
        out_shape=(
            jax.ShapeDtypeStruct((node_count, rows_per_node, col_count), blocks.dtype),
            jax.ShapeDtypeStruct((node_count, HUB_PAD, col_count), blocks.dtype),
        ),
        grid_spec=pltpu.PrefetchScalarGridSpec(
            num_scalar_prefetch=3,
            grid=(1,),
            in_specs=[
                pl.BlockSpec(memory_space=pltpu.VMEM),
                pl.BlockSpec(memory_space=pltpu.VMEM),
            ],
            out_specs=(
                pl.BlockSpec(memory_space=pltpu.VMEM),
                pl.BlockSpec(memory_space=pltpu.VMEM),
            ),
            scratch_shapes=[pltpu.SMEM((node_count,), jnp.int32)],
        ),
    )(destination, sources, hubs, tiles, blocks)


def aggregate(
    inputs,
    degree,
    hub_ids,
    hub_adjacency,
    local_rows,
    local_cols,
    local_tiles,
    out_src,
    out_tiles,
    destination,
    landing,
    anchor,
):
    vertex_count, col_count = inputs.shape
    tile_side = local_tiles.shape[1]
    block_count = vertex_count // tile_side
    node_count = lax.axis_size("dom")
    slot_count = landing.shape[1]
    capacity = slot_count // node_count
    hub_count = hub_ids.shape[0]
    blocks = inputs.reshape(block_count, tile_side, col_count)
    block_ids = jnp.arange(block_count, dtype=jnp.int32)
    payload = build_payload(
        destination, out_src.astype(jnp.int32), hub_ids.astype(jnp.int32), out_tiles, blocks,
        node_count, capacity,
    )
    if anchor is not None:
        payload, anchor = lax.optimization_barrier((payload, anchor))
    tiles_in, hubs_in = lax.all_to_all(payload, "dom", split_axis=0, concat_axis=0, tiled=True)
    tiles_in = tiles_in.reshape(slot_count, tile_side, col_count)
    hub_rows = hubs_in[:, :hub_count, :].reshape(node_count * hub_count, col_count)
    from_peers = jnp.einsum(
        "bk,krd->brd", landing, tiles_in, preferred_element_type=jnp.float32
    )
    local_products = jnp.einsum(
        "trs,tsd->trd", local_tiles, blocks[local_cols], preferred_element_type=jnp.float32
    )
    onehot = (local_rows[None, :] == block_ids[:, None]).astype(jnp.float32)
    from_local = jnp.einsum("bt,trd->brd", onehot, local_products, precision=lax.Precision.HIGHEST)
    from_hubs = jnp.dot(hub_adjacency, hub_rows, preferred_element_type=jnp.float32)
    summed = (from_peers + from_local).reshape(vertex_count, col_count) + from_hubs
    return (summed / degree.astype(jnp.float32)[:, None]).astype(jnp.bfloat16), anchor


def feat_to_rows(block):
    feat_count = lax.axis_size("feat")
    row_count, col_count = block.shape
    pieces = block.reshape(feat_count, row_count // feat_count, col_count)
    gathered = lax.all_to_all(pieces, "feat", split_axis=0, concat_axis=0, tiled=True)
    return gathered.transpose(1, 0, 2).reshape(row_count // feat_count, feat_count * col_count)


def rows_to_feat(rows):
    feat_count = lax.axis_size("feat")
    row_count, width = rows.shape
    pieces = rows.reshape(row_count, feat_count, width // feat_count).transpose(1, 0, 2)
    gathered = lax.all_to_all(pieces, "feat", split_axis=0, concat_axis=0, tiled=True)
    return gathered.reshape(feat_count * row_count, width // feat_count)


def mix(own_rows, neigh_rows, self_weight, neigh_weight, gain):
    width = self_weight.shape[1]
    running = jnp.dot(own_rows, self_weight, preferred_element_type=jnp.float32)
    mixed = running + jnp.dot(neigh_rows, neigh_weight, preferred_element_type=jnp.float32)
    rectified = jnp.maximum(mixed, 0.0)
    squares = jnp.sum(rectified * rectified, axis=1, keepdims=True)
    scaled = gain.astype(jnp.float32)[None, :] * rectified * lax.rsqrt(squares / width + EPSILON)
    return scaled.astype(jnp.bfloat16)


def gather_weights(w_self, w_neigh, gains):
    feat_count = lax.axis_size("feat")
    layer_count, depth, slice_width = w_self.shape
    gain_rows = jnp.zeros((layer_count, HUB_PAD, slice_width), gains.dtype).at[:, 0, :].set(gains)
    stacked = jnp.concatenate([w_self, w_neigh, gain_rows], axis=1)
    pieces = [stacked]
    for shift in range(1, feat_count):
        pairs = [(source, (source + shift) % feat_count) for source in range(feat_count)]
        pieces.append(lax.ppermute(stacked, "feat", pairs))
    full = jnp.concatenate(pieces, axis=2)
    return full[:, :depth], full[:, depth : 2 * depth], full[:, 2 * depth]


def natural_columns(shifted):
    feat_count = lax.axis_size("feat")
    row_count, width = shifted.shape
    order = (lax.axis_index("feat") - jnp.arange(feat_count, dtype=jnp.int32)) % feat_count
    blocks = shifted.reshape(row_count, feat_count, width // feat_count)
    return jnp.take(blocks, order, axis=1).reshape(row_count, width)


def per_device(
    features,
    degree,
    hub_ids,
    hub_adjacency,
    local_rows,
    local_cols,
    local_tiles,
    out_dest,
    out_src,
    out_tiles,
    recv_target,
    w_self,
    w_neigh,
    gains,
):
    tile_side = local_tiles.shape[1]
    destination, landing = routing(
        out_dest, recv_target, features.shape[0] // tile_side, lax.axis_size("dom")
    )
    full_self, full_neigh, full_gains = gather_weights(w_self, w_neigh, gains)
    current = features
    own_rows = feat_to_rows(features)
    for layer_idx in range(w_self.shape[0]):
        neighbours, anchored = aggregate(
            current,
            degree,
            hub_ids,
            hub_adjacency,
            local_rows,
            local_cols,
            local_tiles,
            out_src,
            out_tiles,
            destination,
            landing,
            own_rows if layer_idx == 0 else None,
        )
        if anchored is not None:
            own_rows = anchored
        neigh_rows = feat_to_rows(neighbours)
        own_rows = natural_columns(
            mix(
                own_rows,
                neigh_rows,
                full_self[layer_idx],
                full_neigh[layer_idx],
                full_gains[layer_idx],
            )
        )
        current = rows_to_feat(own_rows)
    return current


def solution(mesh):
    in_specs = (
        P("dom", "feat"),
        P("dom"),
        P("dom"),
        P("dom", None),
        P("dom"),
        P("dom"),
        P("dom", None, None),
        P("dom", None),
        P("dom"),
        P("dom", None, None),
        P("dom", None, None),
        P(None, None, "feat"),
        P(None, None, "feat"),
        P(None, "feat"),
    )
    out_specs = P("dom", "feat")
    return jax.shard_map(
        per_device, mesh=mesh, in_specs=in_specs, out_specs=out_specs, check_vma=False
    )
```

```python
import jax
import jax.numpy as jnp
from jax import lax
from jax.experimental import pallas as pl
from jax.experimental.pallas import tpu as pltpu
from jax.sharding import PartitionSpec as P

EPSILON = 1e-06
HUB_PAD = 8
WINDOW = 16


def routing(out_dest, recv_target, block_count, node_count):
    targets = recv_target[0].reshape(-1)
    block_ids = jnp.arange(block_count, dtype=jnp.int32)
    landing = (targets[None, :] == block_ids[:, None]).astype(jnp.bfloat16)
    return out_dest[:, 0].astype(jnp.int32), landing


def payload_kernel(dest_ref, src_ref, hub_ref, tiles_ref, blocks_ref, out_ref, counts_ref):
    node_count, rows_per_node, col_count = out_ref.shape
    tile_count, tile_side, _ = tiles_ref.shape
    tail = rows_per_node - HUB_PAD
    capacity = tail // tile_side

    def clear(node, carry):
        counts_ref[node] = 0
        return carry

    lax.fori_loop(0, node_count, clear, 0, unroll=8)
    window_rows = lax.broadcasted_iota(jnp.int32, (WINDOW, col_count), 0)
    lanes = lax.broadcasted_iota(jnp.int32, (HUB_PAD, col_count), 0)
    hub = jnp.zeros((HUB_PAD, col_count), jnp.float32)
    for index in range(hub_ref.shape[0]):
        vertex = hub_ref[index]
        block = vertex // tile_side
        row = vertex % tile_side
        start = pl.multiple_of((row // WINDOW) * WINDOW, WINDOW)
        window = blocks_ref[block, pl.ds(start, WINDOW), :].astype(jnp.float32)
        picked = jnp.sum(jnp.where(window_rows == row % WINDOW, window, 0.0), axis=0, keepdims=True)
        hub = jnp.where(lanes == index, picked, hub)
    hub = hub.astype(out_ref.dtype)

    def put_hub(node, carry):
        out_ref[node, pl.ds(tail, HUB_PAD), :] = hub
        return carry

    lax.fori_loop(0, node_count, put_hub, 0, unroll=8)

    def put_tile(tile, carry):
        node = dest_ref[tile]
        rank = counts_ref[node]
        counts_ref[node] = rank + 1
        first = pl.multiple_of(jnp.minimum(rank, capacity - 1) * tile_side, tile_side)
        product = jnp.dot(
            tiles_ref[tile], blocks_ref[src_ref[tile]], preferred_element_type=jnp.float32
        )
        out_ref[node, pl.ds(first, tile_side), :] = product.astype(out_ref.dtype)
        return carry

    lax.fori_loop(0, tile_count, put_tile, 0, unroll=8)
    empty = jnp.zeros((tile_side, col_count), out_ref.dtype)

    def clear_unused(node, carry):
        filled = counts_ref[node]
        for slot in range(capacity):
            @pl.when(filled <= slot)
            def _():
                out_ref[node, pl.ds(slot * tile_side, tile_side), :] = empty
        return carry

    lax.fori_loop(0, node_count, clear_unused, 0, unroll=8)


def build_payload(destination, sources, hubs, tiles, blocks, node_count, capacity):
    tile_side = tiles.shape[1]
    col_count = blocks.shape[2]
    rows_per_node = capacity * tile_side + HUB_PAD
    return pl.pallas_call(
        payload_kernel,
        out_shape=jax.ShapeDtypeStruct((node_count, rows_per_node, col_count), blocks.dtype),
        grid_spec=pltpu.PrefetchScalarGridSpec(
            num_scalar_prefetch=3,
            grid=(1,),
            in_specs=[
                pl.BlockSpec(memory_space=pltpu.VMEM),
                pl.BlockSpec(memory_space=pltpu.VMEM),
            ],
            out_specs=pl.BlockSpec(memory_space=pltpu.VMEM),
            scratch_shapes=[pltpu.SMEM((node_count,), jnp.int32)],
        ),
    )(destination, sources, hubs, tiles, blocks)


def aggregate(
    inputs,
    degree,
    hub_ids,
    hub_adjacency,
    local_rows,
    local_cols,
    local_tiles,
    out_src,
    out_tiles,
    destination,
    landing,
    anchor,
):
    vertex_count, col_count = inputs.shape
    tile_side = local_tiles.shape[1]
    block_count = vertex_count // tile_side
    node_count = lax.axis_size("dom")
    slot_count = landing.shape[1]
    capacity = slot_count // node_count
    hub_count = hub_ids.shape[0]
    blocks = inputs.reshape(block_count, tile_side, col_count)
    block_ids = jnp.arange(block_count, dtype=jnp.int32)
    payload = build_payload(
        destination, out_src.astype(jnp.int32), hub_ids.astype(jnp.int32), out_tiles, blocks,
        node_count, capacity,
    )
    if anchor is not None:
        payload, anchor = lax.optimization_barrier((payload, anchor))
    arrived = lax.all_to_all(payload, "dom", split_axis=0, concat_axis=0, tiled=True)
    tiles_in = arrived[:, : capacity * tile_side, :].reshape(slot_count, tile_side, col_count)
    hub_rows = arrived[:, capacity * tile_side : capacity * tile_side + hub_count, :].reshape(
        node_count * hub_count, col_count
    )
    from_peers = jnp.einsum(
        "bk,krd->brd", landing, tiles_in, preferred_element_type=jnp.float32
    )
    local_products = jnp.einsum(
        "trs,tsd->trd", local_tiles, blocks[local_cols], preferred_element_type=jnp.float32
    )
    onehot = (local_rows[None, :] == block_ids[:, None]).astype(jnp.float32)
    from_local = jnp.einsum("bt,trd->brd", onehot, local_products, precision=lax.Precision.HIGHEST)
    from_hubs = jnp.dot(hub_adjacency, hub_rows, preferred_element_type=jnp.float32)
    summed = (from_peers + from_local).reshape(vertex_count, col_count) + from_hubs
    return (summed / degree.astype(jnp.float32)[:, None]).astype(jnp.bfloat16), anchor


def feat_to_rows(block):
    feat_count = lax.axis_size("feat")
    row_count, col_count = block.shape
    pieces = block.reshape(feat_count, row_count // feat_count, col_count)
    gathered = lax.all_to_all(pieces, "feat", split_axis=0, concat_axis=0, tiled=True)
    return gathered.transpose(1, 0, 2).reshape(row_count // feat_count, feat_count * col_count)


def rows_to_feat(rows):
    feat_count = lax.axis_size("feat")
    row_count, width = rows.shape
    pieces = rows.reshape(row_count, feat_count, width // feat_count).transpose(1, 0, 2)
    gathered = lax.all_to_all(pieces, "feat", split_axis=0, concat_axis=0, tiled=True)
    return gathered.reshape(feat_count * row_count, width // feat_count)


def mix(own_rows, neigh_rows, self_weight, neigh_weight, gain):
    width = self_weight.shape[1]
    running = jnp.dot(own_rows, self_weight, preferred_element_type=jnp.float32)
    mixed = running + jnp.dot(neigh_rows, neigh_weight, preferred_element_type=jnp.float32)
    rectified = jnp.maximum(mixed, 0.0)
    squares = jnp.sum(rectified * rectified, axis=1, keepdims=True)
    scaled = gain.astype(jnp.float32)[None, :] * rectified * lax.rsqrt(squares / width + EPSILON)
    return scaled.astype(jnp.bfloat16)


def gather_weights(w_self, w_neigh, gains):
    feat_count = lax.axis_size("feat")
    layer_count, depth, slice_width = w_self.shape
    gain_rows = jnp.zeros((layer_count, HUB_PAD, slice_width), gains.dtype).at[:, 0, :].set(gains)
    stacked = jnp.concatenate([w_self, w_neigh, gain_rows], axis=1)
    pieces = [stacked]
    for shift in range(1, feat_count):
        pairs = [(source, (source + shift) % feat_count) for source in range(feat_count)]
        pieces.append(lax.ppermute(stacked, "feat", pairs))
    full = jnp.concatenate(pieces, axis=2)
    return full[:, :depth], full[:, depth : 2 * depth], full[:, 2 * depth]


def natural_columns(shifted):
    feat_count = lax.axis_size("feat")
    row_count, width = shifted.shape
    order = (lax.axis_index("feat") - jnp.arange(feat_count, dtype=jnp.int32)) % feat_count
    blocks = shifted.reshape(row_count, feat_count, width // feat_count)
    return jnp.take(blocks, order, axis=1).reshape(row_count, width)


def per_device(
    features,
    degree,
    hub_ids,
    hub_adjacency,
    local_rows,
    local_cols,
    local_tiles,
    out_dest,
    out_src,
    out_tiles,
    recv_target,
    w_self,
    w_neigh,
    gains,
):
    tile_side = local_tiles.shape[1]
    destination, landing = routing(
        out_dest, recv_target, features.shape[0] // tile_side, lax.axis_size("dom")
    )
    full_self, full_neigh, full_gains = gather_weights(w_self, w_neigh, gains)
    current = features
    own_rows = feat_to_rows(features)
    for layer_idx in range(w_self.shape[0]):
        neighbours, anchored = aggregate(
            current,
            degree,
            hub_ids,
            hub_adjacency,
            local_rows,
            local_cols,
            local_tiles,
            out_src,
            out_tiles,
            destination,
            landing,
            own_rows if layer_idx == 0 else None,
        )
        if anchored is not None:
            own_rows = anchored
        neigh_rows = feat_to_rows(neighbours)
        own_rows = natural_columns(
            mix(
                own_rows,
                neigh_rows,
                full_self[layer_idx],
                full_neigh[layer_idx],
                full_gains[layer_idx],
            )
        )
        current = rows_to_feat(own_rows)
    return current


def solution(mesh):
    in_specs = (
        P("dom", "feat"),
        P("dom"),
        P("dom"),
        P("dom", None),
        P("dom"),
        P("dom"),
        P("dom", None, None),
        P("dom", None),
        P("dom"),
        P("dom", None, None),
        P("dom", None, None),
        P(None, None, "feat"),
        P(None, None, "feat"),
        P(None, "feat"),
    )
    out_specs = P("dom", "feat")
    return jax.shard_map(
        per_device, mesh=mesh, in_specs=in_specs, out_specs=out_specs, check_vma=False
    )
```

```python
import jax
import jax.numpy as jnp
from jax import lax
from jax.experimental import pallas as pl
from jax.experimental.pallas import tpu as pltpu
from jax.sharding import PartitionSpec as P

EPSILON = 1e-06
HUB_PAD = 8
WINDOW = 16


def routing(out_dest, recv_target, block_count, node_count):
    targets = recv_target[0].reshape(-1)
    block_ids = jnp.arange(block_count, dtype=jnp.int32)
    landing = (targets[None, :] == block_ids[:, None]).astype(jnp.bfloat16)
    return out_dest[:, 0].astype(jnp.int32), landing


def payload_kernel(dest_ref, src_ref, hub_ref, tiles_ref, blocks_ref, out_ref, counts_ref):
    node_count, rows_per_node, col_count = out_ref.shape
    tile_count, tile_side, _ = tiles_ref.shape
    tail = rows_per_node - HUB_PAD
    capacity = tail // tile_side
    out_ref[...] = jnp.zeros(out_ref.shape, out_ref.dtype)

    def clear(node, carry):
        counts_ref[node] = 0
        return carry

    lax.fori_loop(0, node_count, clear, 0, unroll=8)
    window_rows = lax.broadcasted_iota(jnp.int32, (WINDOW, col_count), 0)
    lanes = lax.broadcasted_iota(jnp.int32, (HUB_PAD, col_count), 0)
    hub = jnp.zeros((HUB_PAD, col_count), jnp.float32)
    for index in range(hub_ref.shape[0]):
        vertex = hub_ref[index]
        block = vertex // tile_side
        row = vertex % tile_side
        start = pl.multiple_of((row // WINDOW) * WINDOW, WINDOW)
        window = blocks_ref[block, pl.ds(start, WINDOW), :].astype(jnp.float32)
        picked = jnp.sum(jnp.where(window_rows == row % WINDOW, window, 0.0), axis=0, keepdims=True)
        hub = jnp.where(lanes == index, picked, hub)
    hub = hub.astype(out_ref.dtype)

    def put_hub(node, carry):
        out_ref[node, pl.ds(tail, HUB_PAD), :] = hub
        return carry

    lax.fori_loop(0, node_count, put_hub, 0, unroll=8)

    def put_tile(tile, carry):
        node = dest_ref[tile]
        rank = counts_ref[node]
        counts_ref[node] = rank + 1
        first = pl.multiple_of(jnp.minimum(rank, capacity - 1) * tile_side, tile_side)
        product = jnp.dot(
            tiles_ref[tile], blocks_ref[src_ref[tile]], preferred_element_type=jnp.float32
        )
        out_ref[node, pl.ds(first, tile_side), :] = product.astype(out_ref.dtype)
        return carry

    lax.fori_loop(0, tile_count, put_tile, 0, unroll=8)


def build_payload(destination, sources, hubs, tiles, blocks, node_count, capacity):
    tile_side = tiles.shape[1]
    col_count = blocks.shape[2]
    rows_per_node = capacity * tile_side + HUB_PAD
    return pl.pallas_call(
        payload_kernel,
        out_shape=jax.ShapeDtypeStruct((node_count, rows_per_node, col_count), blocks.dtype),
        grid_spec=pltpu.PrefetchScalarGridSpec(
            num_scalar_prefetch=3,
            grid=(1,),
            in_specs=[
                pl.BlockSpec(memory_space=pltpu.VMEM),
                pl.BlockSpec(memory_space=pltpu.VMEM),
            ],
            out_specs=pl.BlockSpec(memory_space=pltpu.VMEM),
            scratch_shapes=[pltpu.SMEM((node_count,), jnp.int32)],
        ),
    )(destination, sources, hubs, tiles, blocks)


def aggregate(
    inputs,
    degree,
    hub_ids,
    hub_adjacency,
    local_rows,
    local_cols,
    local_tiles,
    out_src,
    out_tiles,
    destination,
    landing,
    anchor,
):
    vertex_count, col_count = inputs.shape
    tile_side = local_tiles.shape[1]
    block_count = vertex_count // tile_side
    node_count = lax.axis_size("dom")
    slot_count = landing.shape[1]
    capacity = slot_count // node_count
    hub_count = hub_ids.shape[0]
    blocks = inputs.reshape(block_count, tile_side, col_count)
    block_ids = jnp.arange(block_count, dtype=jnp.int32)
    payload = build_payload(
        destination, out_src.astype(jnp.int32), hub_ids.astype(jnp.int32), out_tiles, blocks,
        node_count, capacity,
    )
    if anchor is not None:
        payload, anchor = lax.optimization_barrier((payload, anchor))
    arrived = lax.all_to_all(payload, "dom", split_axis=0, concat_axis=0, tiled=True)
    tiles_in = arrived[:, : capacity * tile_side, :].reshape(slot_count, tile_side, col_count)
    hub_rows = arrived[:, capacity * tile_side : capacity * tile_side + hub_count, :].reshape(
        node_count * hub_count, col_count
    )
    from_peers = jnp.einsum(
        "bk,krd->brd", landing, tiles_in, preferred_element_type=jnp.float32
    )
    local_products = jnp.einsum(
        "trs,tsd->trd", local_tiles, blocks[local_cols], preferred_element_type=jnp.float32
    )
    onehot = (local_rows[None, :] == block_ids[:, None]).astype(jnp.float32)
    from_local = jnp.einsum("bt,trd->brd", onehot, local_products, precision=lax.Precision.HIGHEST)
    from_hubs = jnp.dot(hub_adjacency, hub_rows, preferred_element_type=jnp.float32)
    summed = (from_peers + from_local).reshape(vertex_count, col_count) + from_hubs
    return (summed / degree.astype(jnp.float32)[:, None]).astype(jnp.bfloat16), anchor


def feat_to_rows(block):
    feat_count = lax.axis_size("feat")
    row_count, col_count = block.shape
    pieces = block.reshape(feat_count, row_count // feat_count, col_count)
    gathered = lax.all_to_all(pieces, "feat", split_axis=0, concat_axis=0, tiled=True)
    return gathered.transpose(1, 0, 2).reshape(row_count // feat_count, feat_count * col_count)


def rows_to_feat(rows):
    feat_count = lax.axis_size("feat")
    row_count, width = rows.shape
    pieces = rows.reshape(row_count, feat_count, width // feat_count).transpose(1, 0, 2)
    gathered = lax.all_to_all(pieces, "feat", split_axis=0, concat_axis=0, tiled=True)
    return gathered.reshape(feat_count * row_count, width // feat_count)


def mix(own_rows, neigh_rows, self_weight, neigh_weight, gain):
    width = self_weight.shape[1]
    running = jnp.dot(own_rows, self_weight, preferred_element_type=jnp.float32)
    mixed = running + jnp.dot(neigh_rows, neigh_weight, preferred_element_type=jnp.float32)
    rectified = jnp.maximum(mixed, 0.0)
    squares = jnp.sum(rectified * rectified, axis=1, keepdims=True)
    scaled = gain.astype(jnp.float32)[None, :] * rectified * lax.rsqrt(squares / width + EPSILON)
    return scaled.astype(jnp.bfloat16)


def gather_weights(w_self, w_neigh, gains):
    feat_count = lax.axis_size("feat")
    layer_count, depth, slice_width = w_self.shape
    gain_rows = jnp.zeros((layer_count, HUB_PAD, slice_width), gains.dtype).at[:, 0, :].set(gains)
    stacked = jnp.concatenate([w_self, w_neigh, gain_rows], axis=1)
    pieces = [stacked]
    for shift in range(1, feat_count):
        pairs = [(source, (source + shift) % feat_count) for source in range(feat_count)]
        pieces.append(lax.ppermute(stacked, "feat", pairs))
    full = jnp.concatenate(pieces, axis=2)
    return full[:, :depth], full[:, depth : 2 * depth], full[:, 2 * depth]


def natural_columns(shifted):
    feat_count = lax.axis_size("feat")
    row_count, width = shifted.shape
    order = (lax.axis_index("feat") - jnp.arange(feat_count, dtype=jnp.int32)) % feat_count
    blocks = shifted.reshape(row_count, feat_count, width // feat_count)
    return jnp.take(blocks, order, axis=1).reshape(row_count, width)


def per_device(
    features,
    degree,
    hub_ids,
    hub_adjacency,
    local_rows,
    local_cols,
    local_tiles,
    out_dest,
    out_src,
    out_tiles,
    recv_target,
    w_self,
    w_neigh,
    gains,
):
    tile_side = local_tiles.shape[1]
    destination, landing = routing(
        out_dest, recv_target, features.shape[0] // tile_side, lax.axis_size("dom")
    )
    full_self, full_neigh, full_gains = gather_weights(w_self, w_neigh, gains)
    current = features
    own_rows = feat_to_rows(features)
    for layer_idx in range(w_self.shape[0]):
        neighbours, anchored = aggregate(
            current,
            degree,
            hub_ids,
            hub_adjacency,
            local_rows,
            local_cols,
            local_tiles,
            out_src,
            out_tiles,
            destination,
            landing,
            None,
        )
        if anchored is not None:
            own_rows = anchored
        neigh_rows = feat_to_rows(neighbours)
        own_rows = natural_columns(
            mix(
                own_rows,
                neigh_rows,
                full_self[layer_idx],
                full_neigh[layer_idx],
                full_gains[layer_idx],
            )
        )
        current = rows_to_feat(own_rows)
    return current


def solution(mesh):
    in_specs = (
        P("dom", "feat"),
        P("dom"),
        P("dom"),
        P("dom", None),
        P("dom"),
        P("dom"),
        P("dom", None, None),
        P("dom", None),
        P("dom"),
        P("dom", None, None),
        P("dom", None, None),
        P(None, None, "feat"),
        P(None, None, "feat"),
        P(None, "feat"),
    )
    out_specs = P("dom", "feat")
    return jax.shard_map(
        per_device, mesh=mesh, in_specs=in_specs, out_specs=out_specs, check_vma=False
    )
```
